512 devices in a mesh: dp: 4 (over y_lo, core), seq: 4 (over x), fsdp: 32 (over y_hi, z).
Axes of the slice: x: 4, y: 8 (y_hi: 4, y_lo: 2; y = y_hi * 2 + y_lo), z: 8, core: 2. Of those that a mesh axis runs over, the one named last changes fastest.
Arguments:
- patches: bfloat16 [128, 768, 6144], P(('dp', 'fsdp'), 'seq'), may hold values from -100 to 100
- segments: int32 [128, 768], P(('dp', 'fsdp'), 'seq'), may hold values from 0 to 7, never falling along the last dimension, each value on 1 to 384 neighbouring positions
- qkv_weight: bfloat16 [6144, 384], P('fsdp'), may hold values from -0.078125 to 0.078125
- cotangent: bfloat16 [128, 768, 128], P(('dp', 'fsdp'), 'seq'), may hold values from -6 to 6
Outputs:
- input_grad: bfloat16 [128, 768, 6144], P(('dp', 'fsdp'), 'seq')
- weight_grad: float32 [6144, 384], P('fsdp')
The draws below stay inside these ranges and needn't reach their ends.
Inputs may be any that keep to these rules, and one draw needn't show every extreme that they name: `segments`: within a sequence the image number never falls; each of the 8 images has 1 to 384 patches and one has exactly 384.
All inputs are finite; a program needn't handle non-finite values.
Results may differ from the reference program's by a relative error of at most 0.034.
The reference program's roundings to bfloat16 on the way count: a program that leaves them out, or rounds other values in their place, can miss the bound.
Values may be sent and summed in bfloat16 or wider, within the bound.
No kernel may reach another device: no remote copies, remote signals or barrier semaphores. Data moves between devices by JAX's collectives and lax.ppermute only.
A program may use at most 64 MiB of HBM per device.

```python
import math
import jax
import jax.numpy as jnp
import numpy as np
from jax import lax

D = 6144
HD = 128
IMAGES = 8
SEQ_LEN = 768
SEQS = 128


def draw_patches(key, part):
    base_key = jax.random.fold_in(key, 0)
    return jnp.clip(jax.random.normal(base_key, (SEQS, SEQ_LEN, D), jnp.float32), -6.0, 6.0).astype(jnp.bfloat16)


def steps_of(rng, shape, cuts, smallest, high):
    level, own = 1.0, jax.random.fold_in(rng, 6)
    for dim, parts in cuts:
        steps = jnp.exp(jax.random.uniform(jax.random.fold_in(own, dim), (parts,), jnp.float32, smallest / len(cuts), high / len(cuts)))
        level = level * jnp.repeat(steps, shape[dim] // parts).reshape([-1 if axis == dim else 1 for axis in range(len(shape))])
    return level


def split_up(count, total, limit, lean):
    loads = [(1 << 20) // math.isqrt(grade ** lean) + 1 for grade in range(2, count + 1)]
    spare, holding = total - limit - (count - 1), [1] * (count - 1)
    while spare > 0:
        candidates = [i for i in range(count - 1) if holding[i] < limit]
        whole, left = sum([loads[i] for i in candidates]), spare
        for i in candidates:
            addition = min(limit - holding[i], max(1, left * loads[i] // whole), spare)
            holding[i] = holding[i] + addition
            spare = spare - addition
    return np.array([limit] + holding)


def uneven_parts(key, number_of, total, bound, skew):
    if number_of == 2:
        one = jax.random.randint(key, (), max(1, total - bound), min(bound, total - 1) + 1)
        return jnp.stack([one, total - one])
    tallies = jnp.asarray(split_up(number_of, total, bound, skew), jnp.int32)
    couples = (number_of - 1) // 2
    giver, receiver = tallies[1:1 + 2 * couples:2], tallies[2:2 + 2 * couples:2]
    margin = jnp.minimum(giver - 1, bound - receiver)
    passed = jax.random.randint(jax.random.fold_in(key, 1), (couples,), 0, 1 << 20) % (margin + 1)
    tallies = tallies.at[1:1 + 2 * couples:2].set(giver - passed).at[2:2 + 2 * couples:2].set(receiver + passed)
    return tallies[jax.random.permutation(jax.random.fold_in(key, 2), number_of)]


def scatter_about(own_key, shape, scale, most, pieces=(), kind=jnp.bfloat16):
    values = scale * jax.random.normal(own_key, shape, jnp.float32)
    if pieces:
        values = values * steps_of(own_key, shape, pieces, -0.22, 0.18)
    return jnp.clip(values, -most, most).astype(kind)


def setup_inputs(seed: int = 0) -> dict:
    streams_of = jax.random.split(jax.random.key(seed), 5)
    patches = draw_patches(jax.random.fold_in(streams_of[4], 71), 0)
    segments = jax.vmap(lambda own: jnp.searchsorted(jnp.cumsum(uneven_parts(own, IMAGES, SEQ_LEN, SEQ_LEN // 2, 2)), jnp.arange(SEQ_LEN), side="right"))(jax.random.split(streams_of[1], SEQS)).reshape((SEQS, SEQ_LEN)).astype(jnp.int32)
    qkv_weight = scatter_about(streams_of[2], (D, 3 * HD), D ** -0.5, 0.078125, ((0, 32),))
    cotangent = scatter_about(streams_of[3], (SEQS, SEQ_LEN, HD), 1.0, 6.0, ((0, 128), (1, 4)))
    return dict(patches=patches, segments=segments, qkv_weight=qkv_weight, cotangent=cotangent)


def contract_first(left, right):
    return lax.dot_general(left, right, (((0,), (0,)), ((), ())), preferred_element_type=jnp.float32)


def contract_last(left, right):
    return lax.dot_general(left, right, (((1,), (1,)), ((), ())), preferred_element_type=jnp.float32)


def reference(patches, segments, qkv_weight, cotangent):
    scale = HD ** -0.5

    def one_sequence(carried, inputs):
        features, image_ids, grad_out = inputs
        heads = jnp.dot(features, qkv_weight, preferred_element_type=jnp.float32).astype(jnp.bfloat16)
        query = heads[:, :HD]
        keys = heads[:, HD:2 * HD]
        values_head = heads[:, 2 * HD:]
        scores = contract_last(query, keys) * scale
        allowed = image_ids[:, None] == image_ids[None, :]
        highest = jnp.max(jnp.where(allowed, scores, -jnp.inf), axis=1)
        summed = jnp.sum(jnp.where(allowed, jnp.exp(scores - highest[:, None]), 0.0), axis=1)
        log_total = highest + jnp.log(summed)
        attention = jnp.where(allowed, jnp.exp(scores - log_total[:, None]), 0.0)
        attention_low = attention.astype(jnp.bfloat16)
        output = jnp.dot(attention_low, values_head, preferred_element_type=jnp.float32)
        delta_rows = jnp.sum(grad_out.astype(jnp.float32) * output, axis=1)
        grad_value = contract_first(attention_low, grad_out).astype(jnp.bfloat16)
        grad_attention = contract_last(grad_out, values_head)
        grad_scores = (attention * (grad_attention - delta_rows[:, None]) * scale).astype(jnp.bfloat16)
        grad_query = jnp.dot(grad_scores, keys, preferred_element_type=jnp.float32).astype(jnp.bfloat16)
        grad_key = contract_first(grad_scores, query).astype(jnp.bfloat16)
        grad_heads = jnp.concatenate([grad_query, grad_key, grad_value], axis=1)
        input_grad = contract_last(grad_heads, qkv_weight).astype(jnp.bfloat16)
        carried = carried + contract_first(features, grad_heads)
        return carried, input_grad

    start = jnp.zeros((D, 3 * HD), jnp.float32)
    weight_grad, input_grad = lax.scan(one_sequence, start, (patches, segments, cotangent))
    return input_grad, weight_grad
```

```python
import jax
import jax.numpy as jnp
from jax import lax
from jax.sharding import PartitionSpec as P


def contract_first(left, right):
    return lax.dot_general(
        left, right, (((0,), (0,)), ((), ())), preferred_element_type=jnp.float32
    )


def contract_last(left, right):
    return lax.dot_general(
        left, right, (((1,), (1,)), ((), ())), preferred_element_type=jnp.float32
    )


def chip_partner(x):
    pairs = [(i, i ^ 1) for i in range(lax.axis_size("dp"))]
    return lax.ppermute(x, "dp", perm=pairs)


def shards(patches, segments, qkv_weight, cotangent):
    features = patches[0]
    image_ids = segments[0]
    grad_out = cotangent[0]
    width_head = cotangent.shape[2]
    width_all = qkv_weight.shape[1]
    half = width_all // 2
    scale = width_head ** (-0.5)
    core = lax.axis_index("dp") % 2
    first = core == 0

    w_mine = lax.dynamic_slice_in_dim(qkv_weight, core * half, half, axis=1)
    w_mine_all = lax.all_gather(w_mine, "fsdp", axis=0, tiled=True)
    w_other_all = chip_partner(w_mine_all)

    h_mine = jnp.dot(features, w_mine_all, preferred_element_type=jnp.float32)
    h_other = jnp.dot(features, w_other_all, preferred_element_type=jnp.float32)
    projected = jnp.where(
        first,
        jnp.concatenate([h_mine, h_other], axis=1),
        jnp.concatenate([h_other, h_mine], axis=1),
    )
    heads = projected.astype(jnp.bfloat16)
    query = heads[:, :width_head]
    own_pairs = heads[:, width_head:]
    pairs_all, images_all = (
        lax.all_gather(own_pairs, "seq", axis=0, tiled=True),
        lax.all_gather(image_ids, "seq", axis=0, tiled=True),
    )
    keys_all = pairs_all[:, :width_head]
    values_all = pairs_all[:, width_head:]
    scores = contract_last(query, keys_all) * scale
    allowed = image_ids[:, None] == images_all[None, :]
    highest = jnp.max(jnp.where(allowed, scores, -jnp.inf), axis=1)
    summed = jnp.sum(jnp.where(allowed, jnp.exp(scores - highest[:, None]), 0.0), axis=1)
    log_total = highest + jnp.log(summed)
    attention = jnp.where(allowed, jnp.exp(scores - log_total[:, None]), 0.0)
    attention_low = attention.astype(jnp.bfloat16)
    output = jnp.dot(attention_low, values_all, preferred_element_type=jnp.float32)
    delta_rows = jnp.sum(grad_out.astype(jnp.float32) * output, axis=1)
    grad_attention = contract_last(grad_out, values_all)
    grad_scores = (attention * (grad_attention - delta_rows[:, None]) * scale).astype(jnp.bfloat16)
    grad_query = jnp.dot(grad_scores, keys_all, preferred_element_type=jnp.float32).astype(
        jnp.bfloat16
    )
    partial_pairs = jnp.concatenate(
        [contract_first(grad_scores, query), contract_first(attention_low, grad_out)], axis=1
    )
    grad_pairs = lax.psum_scatter(
        partial_pairs.astype(jnp.bfloat16), "seq", scatter_dimension=0, tiled=True
    )
    grad_heads = jnp.concatenate([grad_query, grad_pairs], axis=1)

    g_lo = grad_heads[:, :half]
    g_hi = grad_heads[:, half:]
    g_mine = jnp.where(first, g_lo, g_hi)
    g_other = jnp.where(first, g_hi, g_lo)

    input_grad = (
        contract_last(g_mine, w_mine_all) + contract_last(g_other, w_other_all)
    ).astype(jnp.bfloat16)

    wg_mine = contract_first(features, g_mine)
    wg_other = contract_first(features, g_other)
    wg_from_partner = chip_partner(wg_other.astype(jnp.bfloat16))
    wg_chip = (wg_mine + wg_from_partner.astype(jnp.float32)).astype(jnp.bfloat16)
    wg_rows = lax.psum_scatter(wg_chip, "fsdp", scatter_dimension=0, tiled=True)
    gathered = lax.all_gather(wg_rows, ("dp", "seq"), axis=0, tiled=False).astype(jnp.float32)
    n_dp = lax.axis_size("dp")
    by_dp = gathered.reshape(n_dp, gathered.shape[0] // n_dp, *wg_rows.shape)
    lo = jnp.sum(by_dp[0::2], axis=(0, 1))
    hi = jnp.sum(by_dp[1::2], axis=(0, 1))
    weight_grad = jnp.concatenate([lo, hi], axis=1)
    return (input_grad[None], weight_grad)


def solution(mesh):
    placed = (
        P(("dp", "fsdp"), "seq", None),
        P(("dp", "fsdp"), "seq"),
        P("fsdp", None),
        P(("dp", "fsdp"), "seq", None),
    )
    return jax.shard_map(
        shards,
        mesh=mesh,
        in_specs=placed,
        out_specs=(P(("dp", "fsdp"), "seq", None), P("fsdp", None)),
        check_vma=False,
    )
```

```python
import functools

import jax
import jax.numpy as jnp
from jax import lax
from jax.sharding import PartitionSpec as P


def contract_first(left, right):
    return lax.dot_general(
        left, right, (((0,), (0,)), ((), ())), preferred_element_type=jnp.float32
    )


def contract_last(left, right):
    return lax.dot_general(
        left, right, (((1,), (1,)), ((), ())), preferred_element_type=jnp.float32
    )


def dp_partner(x, bit):
    pairs = [(i, i ^ bit) for i in range(lax.axis_size("dp"))]
    return lax.ppermute(x, "dp", perm=pairs)


class Ring:
    def __init__(self, axis, size, inner):
        self.axis, self.size, self.inner = axis, size, inner

    def total(self):
        return lax.axis_size(self.axis)

    def position(self):
        return (lax.axis_index(self.axis) // self.inner) % self.size

    def shift(self, x, step):
        n, inner, total = self.size, self.inner, self.total()
        pairs = []
        for i in range(total):
            pos = (i // inner) % n
            base = i - pos * inner
            pairs.append((i, base + ((pos + step) % n) * inner))
        return lax.ppermute(x, self.axis, perm=pairs)


def ring_gather(x, ring):
    n = ring.size
    got, slot = [x], {0: 0}
    cw, ccw = x, x
    for t in range(1, n):
        if t % 2 == 1:
            cw = ring.shift(cw, 1)
            slot[(n - (t + 1) // 2) % n] = len(got)
            got.append(cw)
        else:
            ccw = ring.shift(ccw, -1)
            slot[t // 2] = len(got)
            got.append(ccw)
    return jnp.stack(got), [slot[k] for k in range(n)]


def ring_reduce_scatter(blocks, ring):
    n = ring.size
    if n == 1:
        return blocks[0]
    me = ring.position()
    rows = blocks.shape[1]
    upper, lower = blocks[:, : rows // 2], blocks[:, rows // 2 :]

    def pick(part, index):
        return lax.dynamic_index_in_dim(part, index % n, axis=0, keepdims=False)

    acc_cw = pick(upper, me - 1)
    acc_ccw = pick(lower, me + 1)
    for t in range(1, n):
        acc_cw = ring.shift(acc_cw.astype(jnp.bfloat16), 1).astype(jnp.float32) + pick(
            upper, me - 1 - t
        )
        acc_ccw = ring.shift(acc_ccw.astype(jnp.bfloat16), -1).astype(jnp.float32) + pick(
            lower, me + 1 + t
        )
    return jnp.concatenate([acc_cw, acc_ccw], axis=0)


def shards(patches, segments, qkv_weight, cotangent, inner_fsdp):
    features = patches[0]
    image_ids = segments[0]
    grad_out = cotangent[0]
    width_head = cotangent.shape[2]
    width_all = qkv_weight.shape[1]
    rows_w = qkv_weight.shape[0]
    half = width_all // 2
    scale = width_head ** (-0.5)
    core = lax.axis_index("dp") % 2
    first = core == 0
    n_fsdp = lax.axis_size("fsdp")
    outer_fsdp = n_fsdp // inner_fsdp
    ring_y = Ring("fsdp", outer_fsdp, inner_fsdp)
    ring_z = Ring("fsdp", inner_fsdp, 1)
    ring_x = Ring("seq", lax.axis_size("seq"), 1)

    w_mine = lax.dynamic_slice_in_dim(qkv_weight, core * half, half, axis=1)
    stack_y, slot_y = ring_gather(w_mine, ring_y)
    stack_zy, slot_z = ring_gather(stack_y, ring_z)
    flat = stack_zy.reshape(-1, rows_w, half)
    me_y, me_z = ring_y.position(), ring_z.position()
    absolute = jnp.arange(n_fsdp, dtype=jnp.int32)
    rel_y = (absolute // inner_fsdp - me_y) % outer_fsdp
    rel_z = (absolute % inner_fsdp - me_z) % inner_fsdp
    order = jnp.asarray(slot_z, jnp.int32)[rel_z] * outer_fsdp + jnp.asarray(slot_y, jnp.int32)[rel_y]
    w_mine_all = jnp.take(flat, order, axis=0).reshape(n_fsdp * rows_w, half)
    w_other_all = dp_partner(w_mine_all, 1)

    h_mine = jnp.dot(features, w_mine_all, preferred_element_type=jnp.float32)
    h_other = jnp.dot(features, w_other_all, preferred_element_type=jnp.float32)
    projected = jnp.where(
        first,
        jnp.concatenate([h_mine, h_other], axis=1),
        jnp.concatenate([h_other, h_mine], axis=1),
    )
    heads = projected.astype(jnp.bfloat16)
    query = heads[:, :width_head]
    own_pairs = heads[:, width_head:]
    pairs_all, images_all = (
        lax.all_gather(own_pairs, "seq", axis=0, tiled=True),
        lax.all_gather(image_ids, "seq", axis=0, tiled=True),
    )
    keys_all = pairs_all[:, :width_head]
    values_all = pairs_all[:, width_head:]
    scores = contract_last(query, keys_all) * scale
    allowed = image_ids[:, None] == images_all[None, :]
    highest = jnp.max(jnp.where(allowed, scores, -jnp.inf), axis=1)
    summed = jnp.sum(jnp.where(allowed, jnp.exp(scores - highest[:, None]), 0.0), axis=1)
    log_total = highest + jnp.log(summed)
    attention = jnp.where(allowed, jnp.exp(scores - log_total[:, None]), 0.0)
    attention_low = attention.astype(jnp.bfloat16)
    output = jnp.dot(attention_low, values_all, preferred_element_type=jnp.float32)
    delta_rows = jnp.sum(grad_out.astype(jnp.float32) * output, axis=1)
    grad_attention = contract_last(grad_out, values_all)
    grad_scores = (attention * (grad_attention - delta_rows[:, None]) * scale).astype(jnp.bfloat16)
    grad_query = jnp.dot(grad_scores, keys_all, preferred_element_type=jnp.float32).astype(
        jnp.bfloat16
    )
    partial_pairs = jnp.concatenate(
        [contract_first(grad_scores, query), contract_first(attention_low, grad_out)], axis=1
    )
    grad_pairs = lax.psum_scatter(
        partial_pairs.astype(jnp.bfloat16), "seq", scatter_dimension=0, tiled=True
    )
    grad_heads = jnp.concatenate([grad_query, grad_pairs], axis=1)

    g_lo = grad_heads[:, :half]
    g_hi = grad_heads[:, half:]
    g_mine = jnp.where(first, g_lo, g_hi)
    g_other = jnp.where(first, g_hi, g_lo)

    input_grad = (
        contract_last(g_mine, w_mine_all) + contract_last(g_other, w_other_all)
    ).astype(jnp.bfloat16)

    wg_mine = contract_first(features, g_mine)
    wg_other = contract_first(features, g_other)
    wg_from_partner = dp_partner(wg_other.astype(jnp.bfloat16), 1)
    wg_chip = wg_mine + wg_from_partner.astype(jnp.float32)
    blocks = wg_chip.reshape(outer_fsdp, inner_fsdp, rows_w, half)
    over_z = ring_reduce_scatter(jnp.moveaxis(blocks, 1, 0), ring_z)
    over_fsdp = ring_reduce_scatter(over_z, ring_y)

    stack_x, slot_x = ring_gather(over_fsdp, ring_x)
    me_x = ring_x.position()
    n_x = ring_x.size
    rel_x = (jnp.arange(n_x, dtype=jnp.int32) - me_x) % n_x
    in_order = jnp.take(stack_x, jnp.asarray(slot_x, jnp.int32)[rel_x], axis=0)
    over_seq = in_order[0]
    for s in range(1, n_x):
        over_seq = over_seq + in_order[s]
    if lax.axis_size("dp") > 2:
        over_seq = over_seq + dp_partner(over_seq, 2)
    other_half = dp_partner(over_seq, 1)
    weight_grad = jnp.where(
        first,
        jnp.concatenate([over_seq, other_half], axis=1),
        jnp.concatenate([other_half, over_seq], axis=1),
    )
    return (input_grad[None], weight_grad)


def inner_ring_size(mesh):
    axis = mesh.axis_names.index("fsdp")
    line = mesh.devices[tuple(0 if a != axis else slice(None) for a in range(mesh.devices.ndim))]
    line = list(line)
    if not hasattr(line[0], "coords"):
        return len(line)
    count = 1
    while count < len(line) and line[count].coords[1] == line[0].coords[1]:
        count += 1
    return count


def solution(mesh):
    placed = (
        P(("dp", "fsdp"), "seq", None),
        P(("dp", "fsdp"), "seq"),
        P("fsdp", None),
        P(("dp", "fsdp"), "seq", None),
    )
    return jax.shard_map(
        functools.partial(shards, inner_fsdp=inner_ring_size(mesh)),
        mesh=mesh,
        in_specs=placed,
        out_specs=(P(("dp", "fsdp"), "seq", None), P("fsdp", None)),
        check_vma=False,
    )
```

```python
import functools

import jax
import jax.numpy as jnp
from jax import lax
from jax.sharding import PartitionSpec as P


def contract_first(left, right):
    return lax.dot_general(
        left, right, (((0,), (0,)), ((), ())), preferred_element_type=jnp.float32
    )


def contract_last(left, right):
    return lax.dot_general(
        left, right, (((1,), (1,)), ((), ())), preferred_element_type=jnp.float32
    )


def dp_partner(x, bit):
    pairs = [(i, i ^ bit) for i in range(lax.axis_size("dp"))]
    return lax.ppermute(x, "dp", perm=pairs)


class Ring:
    def __init__(self, axis, size, inner):
        self.axis, self.size, self.inner = axis, size, inner

    def total(self):
        return lax.axis_size(self.axis)

    def position(self):
        return (lax.axis_index(self.axis) // self.inner) % self.size

    def shift(self, x, step):
        n, inner, total = self.size, self.inner, self.total()
        pairs = []
        for i in range(total):
            pos = (i // inner) % n
            base = i - pos * inner
            pairs.append((i, base + ((pos + step) % n) * inner))
        return lax.ppermute(x, self.axis, perm=pairs)


def ring_gather(x, ring):
    n = ring.size
    got, slot = [x], {0: 0}
    cw, ccw = x, x
    for t in range(1, n):
        if t % 2 == 1:
            cw = ring.shift(cw, 1)
            slot[(n - (t + 1) // 2) % n] = len(got)
            got.append(cw)
        else:
            ccw = ring.shift(ccw, -1)
            slot[t // 2] = len(got)
            got.append(ccw)
    return jnp.stack(got), [slot[k] for k in range(n)]


def ring_reduce_scatter(blocks, ring, axis=0):
    n = ring.size
    if n == 1:
        return lax.index_in_dim(blocks, 0, axis=axis, keepdims=False)
    me = ring.position()
    split = 1 if axis == 0 else 0
    rows = blocks.shape[split]
    upper = lax.slice_in_dim(blocks, 0, rows // 2, axis=split)
    lower = lax.slice_in_dim(blocks, rows // 2, rows, axis=split)

    def pick(part, index):
        return lax.dynamic_index_in_dim(part, index % n, axis=axis, keepdims=False)

    acc_cw = pick(upper, me - 1)
    acc_ccw = pick(lower, me + 1)
    for t in range(1, n):
        acc_cw = ring.shift(acc_cw.astype(jnp.bfloat16), 1).astype(jnp.float32) + pick(
            upper, me - 1 - t
        )
        acc_ccw = ring.shift(acc_ccw.astype(jnp.bfloat16), -1).astype(jnp.float32) + pick(
            lower, me + 1 + t
        )
    out_split = split - 1 if split > axis else split
    return jnp.concatenate([acc_cw, acc_ccw], axis=out_split)


def shards(patches, segments, qkv_weight, cotangent, inner_fsdp):
    features = patches[0]
    image_ids = segments[0]
    grad_out = cotangent[0]
    width_head = cotangent.shape[2]
    width_all = qkv_weight.shape[1]
    rows_w = qkv_weight.shape[0]
    half = width_all // 2
    scale = width_head ** (-0.5)
    core = lax.axis_index("dp") % 2
    first = core == 0
    n_fsdp = lax.axis_size("fsdp")
    outer_fsdp = n_fsdp // inner_fsdp
    ring_y = Ring("fsdp", outer_fsdp, inner_fsdp)
    ring_z = Ring("fsdp", inner_fsdp, 1)
    ring_x = Ring("seq", lax.axis_size("seq"), 1)

    w_mine = lax.dynamic_slice_in_dim(qkv_weight, core * half, half, axis=1)
    stack_y, slot_y = ring_gather(w_mine, ring_y)
    stack_zy, slot_z = ring_gather(stack_y, ring_z)
    flat = stack_zy.reshape(-1, rows_w, half)
    me_y, me_z = ring_y.position(), ring_z.position()
    absolute = jnp.arange(n_fsdp, dtype=jnp.int32)
    rel_y = (absolute // inner_fsdp - me_y) % outer_fsdp
    rel_z = (absolute % inner_fsdp - me_z) % inner_fsdp
    order = jnp.asarray(slot_z, jnp.int32)[rel_z] * outer_fsdp + jnp.asarray(slot_y, jnp.int32)[rel_y]
    w_mine_all = jnp.take(flat, order, axis=0, mode="clip").reshape(n_fsdp * rows_w, half)
    w_other_all = dp_partner(w_mine_all, 1)

    h_mine = jnp.dot(features, w_mine_all, preferred_element_type=jnp.float32)
    h_other = jnp.dot(features, w_other_all, preferred_element_type=jnp.float32)
    projected = jnp.where(
        first,
        jnp.concatenate([h_mine, h_other], axis=1),
        jnp.concatenate([h_other, h_mine], axis=1),
    )
    heads = projected.astype(jnp.bfloat16)
    n_rows = features.shape[0]
    n_x = ring_x.size
    me_x = ring_x.position()
    ids_col = jnp.broadcast_to(image_ids.astype(jnp.bfloat16)[:, None], (n_rows, width_head))
    packed = jnp.concatenate([heads, grad_out, ids_col], axis=1)
    packed_all = lax.all_gather(packed, "seq", axis=0, tiled=True)
    query_all = packed_all[:, :width_head]
    keys_all = packed_all[:, width_head : 2 * width_head]
    values_all = packed_all[:, 2 * width_head : 3 * width_head]
    grad_out_all = packed_all[:, 3 * width_head : 4 * width_head]
    images_all = packed_all[:, 4 * width_head]
    scores = contract_last(query_all, keys_all) * scale
    allowed = images_all[:, None] == images_all[None, :]
    highest = jnp.max(jnp.where(allowed, scores, -jnp.inf), axis=1)
    summed = jnp.sum(jnp.where(allowed, jnp.exp(scores - highest[:, None]), 0.0), axis=1)
    log_total = highest + jnp.log(summed)
    attention = jnp.where(allowed, jnp.exp(scores - log_total[:, None]), 0.0)
    attention_low = attention.astype(jnp.bfloat16)
    output = jnp.dot(attention_low, values_all, preferred_element_type=jnp.float32)
    delta_rows = jnp.sum(grad_out_all.astype(jnp.float32) * output, axis=1)
    grad_attention = contract_last(grad_out_all, values_all)
    grad_scores = (attention * (grad_attention - delta_rows[:, None]) * scale).astype(jnp.bfloat16)
    start = me_x * n_rows
    own_rows = lax.dynamic_slice_in_dim(grad_scores, start, n_rows, axis=0)
    own_cols = lax.dynamic_slice_in_dim(grad_scores, start, n_rows, axis=1)
    own_attention = lax.dynamic_slice_in_dim(attention_low, start, n_rows, axis=1)
    grad_query = jnp.dot(own_rows, keys_all, preferred_element_type=jnp.float32)
    grad_key = contract_first(own_cols, query_all)
    grad_value = contract_first(own_attention, grad_out_all)
    grad_heads = jnp.concatenate([grad_query, grad_key, grad_value], axis=1).astype(jnp.bfloat16)

    g_lo = grad_heads[:, :half]
    g_hi = grad_heads[:, half:]
    g_mine = jnp.where(first, g_lo, g_hi)
    g_other = jnp.where(first, g_hi, g_lo)

    input_grad = (
        contract_last(g_mine, w_mine_all) + contract_last(g_other, w_other_all)
    ).astype(jnp.bfloat16)

    blocked = features.reshape(n_rows, n_fsdp, rows_w)
    wg_mine = jnp.einsum("pjd,pc->jdc", blocked, g_mine, preferred_element_type=jnp.float32)
    wg_other = jnp.einsum("pjd,pc->jdc", blocked, g_other, preferred_element_type=jnp.float32)
    wg_from_partner = dp_partner(wg_other.astype(jnp.bfloat16), 1)
    wg_chip = wg_mine + wg_from_partner.astype(jnp.float32)
    blocks = wg_chip.reshape(outer_fsdp, inner_fsdp, rows_w, half)
    over_z = ring_reduce_scatter(blocks, ring_z, axis=1)
    over_fsdp = ring_reduce_scatter(over_z, ring_y)

    stack_x, slot_x = ring_gather(over_fsdp, ring_x)
    rel_x = (jnp.arange(n_x, dtype=jnp.int32) - me_x) % n_x
    in_order = jnp.take(stack_x, jnp.asarray(slot_x, jnp.int32)[rel_x], axis=0, mode="clip")
    over_seq = in_order[0]
    for s in range(1, n_x):
        over_seq = over_seq + in_order[s]
    if lax.axis_size("dp") > 2:
        over_seq = over_seq + dp_partner(over_seq, 2)
    other_half = dp_partner(over_seq, 1)
    weight_grad = jnp.where(
        first,
        jnp.concatenate([over_seq, other_half], axis=1),
        jnp.concatenate([other_half, over_seq], axis=1),
    )
    return (input_grad[None], weight_grad)


def inner_ring_size(mesh):
    axis = mesh.axis_names.index("fsdp")
    line = mesh.devices[tuple(0 if a != axis else slice(None) for a in range(mesh.devices.ndim))]
    line = list(line)
    if not hasattr(line[0], "coords"):
        return len(line)
    count = 1
    while count < len(line) and line[count].coords[1] == line[0].coords[1]:
        count += 1
    return count


def solution(mesh):
    placed = (
        P(("dp", "fsdp"), "seq", None),
        P(("dp", "fsdp"), "seq"),
        P("fsdp", None),
        P(("dp", "fsdp"), "seq", None),
    )
    return jax.shard_map(
        functools.partial(shards, inner_fsdp=inner_ring_size(mesh)),
        mesh=mesh,
        in_specs=placed,
        out_specs=(P(("dp", "fsdp"), "seq", None), P("fsdp", None)),
        check_vma=False,
    )
```

```python
import functools

import jax
import jax.numpy as jnp
from jax import lax
from jax.sharding import PartitionSpec as P


def contract_first(left, right):
    return lax.dot_general(
        left, right, (((0,), (0,)), ((), ())), preferred_element_type=jnp.float32
    )


def contract_last(left, right):
    return lax.dot_general(
        left, right, (((1,), (1,)), ((), ())), preferred_element_type=jnp.float32
    )


def dp_partner(x, bit):
    pairs = [(i, i ^ bit) for i in range(lax.axis_size("dp"))]
    return lax.ppermute(x, "dp", perm=pairs)


class Ring:
    def __init__(self, axis, size, inner):
        self.axis, self.size, self.inner = axis, size, inner

    def total(self):
        return lax.axis_size(self.axis)

    def position(self):
        return (lax.axis_index(self.axis) // self.inner) % self.size

    def shift(self, x, step):
        n, inner, total = self.size, self.inner, self.total()
        pairs = []
        for i in range(total):
            pos = (i // inner) % n
            base = i - pos * inner
            pairs.append((i, base + ((pos + step) % n) * inner))
        return lax.ppermute(x, self.axis, perm=pairs)


def ring_gather(x, ring):
    n = ring.size
    got, slot = [x], {0: 0}
    cw, ccw = x, x
    for t in range(1, n):
        if t % 2 == 1:
            cw = ring.shift(cw, 1)
            slot[(n - (t + 1) // 2) % n] = len(got)
            got.append(cw)
        else:
            ccw = ring.shift(ccw, -1)
            slot[t // 2] = len(got)
            got.append(ccw)
    return jnp.stack(got), [slot[k] for k in range(n)]


def ring_reduce_scatter(blocks, ring, axis=0):
    n = ring.size
    me = ring.position()

    def pick(index):
        return lax.dynamic_index_in_dim(blocks, index % n, axis=axis, keepdims=False)

    total = pick(me)
    if n == 1:
        return total
    up, down = n // 2, (n - 1) // 2
    acc = pick(me + up)
    for t in range(1, up + 1):
        acc = ring.shift(acc.astype(jnp.bfloat16), 1).astype(jnp.float32)
        if t < up:
            acc = acc + pick(me + up - t)
    total = total + acc
    if down:
        acc = pick(me - down)
        for t in range(1, down + 1):
            acc = ring.shift(acc.astype(jnp.bfloat16), -1).astype(jnp.float32)
            if t < down:
                acc = acc + pick(me - down + t)
        total = total + acc
    return total


def shards(patches, segments, qkv_weight, cotangent, inner_fsdp):
    features = patches[0]
    image_ids = segments[0]
    grad_out = cotangent[0]
    width_head = cotangent.shape[2]
    width_all = qkv_weight.shape[1]
    rows_w = qkv_weight.shape[0]
    half = width_all // 2
    scale = width_head ** (-0.5)
    core = lax.axis_index("dp") % 2
    first = core == 0
    n_fsdp = lax.axis_size("fsdp")
    outer_fsdp = n_fsdp // inner_fsdp
    ring_y = Ring("fsdp", outer_fsdp, inner_fsdp)
    ring_z = Ring("fsdp", inner_fsdp, 1)
    ring_x = Ring("seq", lax.axis_size("seq"), 1)

    w_mine = lax.dynamic_slice_in_dim(qkv_weight, core * half, half, axis=1)
    stack_y, slot_y = ring_gather(w_mine, ring_y)
    stack_zy, slot_z = ring_gather(stack_y, ring_z)
    flat = stack_zy.reshape(-1, rows_w, half)
    me_y, me_z = ring_y.position(), ring_z.position()
    absolute = jnp.arange(n_fsdp, dtype=jnp.int32)
    rel_y = (absolute // inner_fsdp - me_y) % outer_fsdp
    rel_z = (absolute % inner_fsdp - me_z) % inner_fsdp
    order = jnp.asarray(slot_z, jnp.int32)[rel_z] * outer_fsdp + jnp.asarray(slot_y, jnp.int32)[rel_y]
    w_mine_all = jnp.take(flat, order, axis=0, mode="clip").reshape(n_fsdp * rows_w, half)
    w_other_all = dp_partner(w_mine_all, 1)

    h_mine = jnp.dot(features, w_mine_all, preferred_element_type=jnp.float32)
    h_other = jnp.dot(features, w_other_all, preferred_element_type=jnp.float32)
    projected = jnp.where(
        first,
        jnp.concatenate([h_mine, h_other], axis=1),
        jnp.concatenate([h_other, h_mine], axis=1),
    )
    heads = projected.astype(jnp.bfloat16)
    n_rows = features.shape[0]
    n_x = ring_x.size
    me_x = ring_x.position()
    ids_col = jnp.broadcast_to(image_ids.astype(jnp.bfloat16)[:, None], (n_rows, width_head))
    packed = jnp.concatenate([heads, grad_out, ids_col], axis=1)
    packed_all = lax.all_gather(packed, "seq", axis=0, tiled=True)
    query_all = packed_all[:, :width_head]
    keys_all = packed_all[:, width_head : 2 * width_head]
    values_all = packed_all[:, 2 * width_head : 3 * width_head]
    grad_out_all = packed_all[:, 3 * width_head : 4 * width_head]
    images_all = packed_all[:, 4 * width_head]
    scores = contract_last(query_all, keys_all) * scale
    allowed = images_all[:, None] == images_all[None, :]
    highest = jnp.max(jnp.where(allowed, scores, -jnp.inf), axis=1)
    summed = jnp.sum(jnp.where(allowed, jnp.exp(scores - highest[:, None]), 0.0), axis=1)
    log_total = highest + jnp.log(summed)
    attention = jnp.where(allowed, jnp.exp(scores - log_total[:, None]), 0.0)
    attention_low = attention.astype(jnp.bfloat16)
    output = jnp.dot(attention_low, values_all, preferred_element_type=jnp.float32)
    delta_rows = jnp.sum(grad_out_all.astype(jnp.float32) * output, axis=1)
    grad_attention = contract_last(grad_out_all, values_all)
    grad_scores = (attention * (grad_attention - delta_rows[:, None]) * scale).astype(jnp.bfloat16)
    start = me_x * n_rows
    own_rows = lax.dynamic_slice_in_dim(grad_scores, start, n_rows, axis=0)
    own_cols = lax.dynamic_slice_in_dim(grad_scores, start, n_rows, axis=1)
    own_attention = lax.dynamic_slice_in_dim(attention_low, start, n_rows, axis=1)
    grad_query = jnp.dot(own_rows, keys_all, preferred_element_type=jnp.float32)
    grad_key = contract_first(own_cols, query_all)
    grad_value = contract_first(own_attention, grad_out_all)
    grad_heads = jnp.concatenate([grad_query, grad_key, grad_value], axis=1).astype(jnp.bfloat16)

    g_lo = grad_heads[:, :half]
    g_hi = grad_heads[:, half:]
    g_mine = jnp.where(first, g_lo, g_hi)
    g_other = jnp.where(first, g_hi, g_lo)

    input_grad = (
        contract_last(g_mine, w_mine_all) + contract_last(g_other, w_other_all)
    ).astype(jnp.bfloat16)

    blocked = features.reshape(n_rows, n_fsdp, rows_w)
    wg_mine = jnp.einsum("pjd,pc->jdc", blocked, g_mine, preferred_element_type=jnp.float32)
    wg_other = jnp.einsum("pjd,pc->jdc", blocked, g_other, preferred_element_type=jnp.float32)
    wg_from_partner = dp_partner(wg_other.astype(jnp.bfloat16), 1)
    wg_chip = wg_mine + wg_from_partner.astype(jnp.float32)
    blocks = wg_chip.reshape(outer_fsdp, inner_fsdp, rows_w, half)
    over_z = ring_reduce_scatter(blocks, ring_z, axis=1)
    over_fsdp = ring_reduce_scatter(over_z, ring_y)

    by_seq = lax.all_gather(over_fsdp, "seq", axis=0, tiled=False)
    over_seq = by_seq[0]
    for s_i in range(1, by_seq.shape[0]):
        over_seq = over_seq + by_seq[s_i]
    by_dp = lax.all_gather(over_seq, "dp", axis=0, tiled=False)
    halves = []
    for c in range(2):
        part = by_dp[c]
        for d in range(c + 2, by_dp.shape[0], 2):
            part = part + by_dp[d]
        halves.append(part)
    weight_grad = jnp.concatenate(halves, axis=1)
    return (input_grad[None], weight_grad)


def inner_ring_size(mesh):
    axis = mesh.axis_names.index("fsdp")
    line = mesh.devices[tuple(0 if a != axis else slice(None) for a in range(mesh.devices.ndim))]
    line = list(line)
    if not hasattr(line[0], "coords"):
        return len(line)
    count = 1
    while count < len(line) and line[count].coords[1] == line[0].coords[1]:
        count += 1
    return count


def solution(mesh):
    placed = (
        P(("dp", "fsdp"), "seq", None),
        P(("dp", "fsdp"), "seq"),
        P("fsdp", None),
        P(("dp", "fsdp"), "seq", None),
    )
    return jax.shard_map(
        functools.partial(shards, inner_fsdp=inner_ring_size(mesh)),
        mesh=mesh,
        in_specs=placed,
        out_specs=(P(("dp", "fsdp"), "seq", None), P("fsdp", None)),
        check_vma=False,
    )
```

```python
import functools

import jax
import jax.numpy as jnp
from jax import lax
from jax.sharding import PartitionSpec as P


def contract_first(left, right):
    return lax.dot_general(
        left, right, (((0,), (0,)), ((), ())), preferred_element_type=jnp.float32
    )


def contract_last(left, right):
    return lax.dot_general(
        left, right, (((1,), (1,)), ((), ())), preferred_element_type=jnp.float32
    )


def dp_partner(x, bit):
    pairs = [(i, i ^ bit) for i in range(lax.axis_size("dp"))]
    return lax.ppermute(x, "dp", perm=pairs)


class Ring:
    def __init__(self, axis, size, inner):
        self.axis, self.size, self.inner = axis, size, inner

    def total(self):
        return lax.axis_size(self.axis)

    def position(self):
        return (lax.axis_index(self.axis) // self.inner) % self.size

    def shift(self, x, step):
        n, inner, total = self.size, self.inner, self.total()
        pairs = []
        for i in range(total):
            pos = (i // inner) % n
            base = i - pos * inner
            pairs.append((i, base + ((pos + step) % n) * inner))
        return lax.ppermute(x, self.axis, perm=pairs)


def ring_gather(x, ring):
    n = ring.size
    got, slot = [x], {0: 0}
    cw, ccw = x, x
    for t in range(1, n):
        if t % 2 == 1:
            cw = ring.shift(cw, 1)
            slot[(n - (t + 1) // 2) % n] = len(got)
            got.append(cw)
        else:
            ccw = ring.shift(ccw, -1)
            slot[t // 2] = len(got)
            got.append(ccw)
    return jnp.stack(got), [slot[k] for k in range(n)]


def ring_reduce_scatter(blocks, ring, axis=0):
    n = ring.size
    me = ring.position()

    def pick(index):
        return lax.dynamic_index_in_dim(blocks, index % n, axis=axis, keepdims=False)

    total = pick(me)
    if n == 1:
        return total
    up, down = n // 2, (n - 1) // 2
    acc = pick(me + up)
    for t in range(1, up + 1):
        acc = ring.shift(acc.astype(jnp.bfloat16), 1).astype(jnp.float32)
        if t < up:
            acc = acc + pick(me + up - t)
    total = total + acc
    if down:
        acc = pick(me - down)
        for t in range(1, down + 1):
            acc = ring.shift(acc.astype(jnp.bfloat16), -1).astype(jnp.float32)
            if t < down:
                acc = acc + pick(me - down + t)
        total = total + acc
    return total


def shards(patches, segments, qkv_weight, cotangent, inner_fsdp):
    features = patches[0]
    image_ids = segments[0]
    grad_out = cotangent[0]
    width_head = cotangent.shape[2]
    width_all = qkv_weight.shape[1]
    rows_w = qkv_weight.shape[0]
    half = width_all // 2
    scale = width_head ** (-0.5)
    core = lax.axis_index("dp") % 2
    first = core == 0
    n_fsdp = lax.axis_size("fsdp")
    outer_fsdp = n_fsdp // inner_fsdp
    ring_y = Ring("fsdp", outer_fsdp, inner_fsdp)
    ring_z = Ring("fsdp", inner_fsdp, 1)
    ring_x = Ring("seq", lax.axis_size("seq"), 1)

    w_mine = lax.dynamic_slice_in_dim(qkv_weight, core * half, half, axis=1)
    stack_y, slot_y = ring_gather(w_mine, ring_y)
    stack_zy, slot_z = ring_gather(stack_y, ring_z)
    flat = stack_zy.reshape(-1, rows_w, half)
    me_y, me_z = ring_y.position(), ring_z.position()
    absolute = jnp.arange(n_fsdp, dtype=jnp.int32)
    rel_y = (absolute // inner_fsdp - me_y) % outer_fsdp
    rel_z = (absolute % inner_fsdp - me_z) % inner_fsdp
    order = jnp.asarray(slot_z, jnp.int32)[rel_z] * outer_fsdp + jnp.asarray(slot_y, jnp.int32)[rel_y]
    w_mine_all = jnp.take(flat, order, axis=0, mode="clip").reshape(n_fsdp * rows_w, half)
    w_other_all = dp_partner(w_mine_all, 1)

    h_mine = jnp.dot(features, w_mine_all, preferred_element_type=jnp.float32)
    h_other = jnp.dot(features, w_other_all, preferred_element_type=jnp.float32)
    projected = jnp.where(
        first,
        jnp.concatenate([h_mine, h_other], axis=1),
        jnp.concatenate([h_other, h_mine], axis=1),
    )
    heads = projected.astype(jnp.bfloat16)
    n_rows = features.shape[0]
    n_x = ring_x.size
    me_x = ring_x.position()
    ids_col = jnp.broadcast_to(image_ids.astype(jnp.bfloat16)[:, None], (n_rows, width_head))
    packed = jnp.concatenate([heads, grad_out, ids_col], axis=1)
    packed_all = lax.all_gather(packed, "seq", axis=0, tiled=True)
    query_all = packed_all[:, :width_head]
    keys_all = packed_all[:, width_head : 2 * width_head]
    values_all = packed_all[:, 2 * width_head : 3 * width_head]
    grad_out_all = packed_all[:, 3 * width_head : 4 * width_head]
    images_all = packed_all[:, 4 * width_head]
    scores = contract_last(query_all, keys_all) * scale
    allowed = images_all[:, None] == images_all[None, :]
    highest = jnp.max(jnp.where(allowed, scores, -jnp.inf), axis=1)
    summed = jnp.sum(jnp.where(allowed, jnp.exp(scores - highest[:, None]), 0.0), axis=1)
    log_total = highest + jnp.log(summed)
    attention = jnp.where(allowed, jnp.exp(scores - log_total[:, None]), 0.0)
    attention_low = attention.astype(jnp.bfloat16)
    output = jnp.dot(attention_low, values_all, preferred_element_type=jnp.float32)
    delta_rows = jnp.sum(grad_out_all.astype(jnp.float32) * output, axis=1)
    grad_attention = contract_last(grad_out_all, values_all)
    grad_scores = (attention * (grad_attention - delta_rows[:, None]) * scale).astype(jnp.bfloat16)
    start = me_x * n_rows
    own_rows = lax.dynamic_slice_in_dim(grad_scores, start, n_rows, axis=0)
    own_cols = lax.dynamic_slice_in_dim(grad_scores, start, n_rows, axis=1)
    own_attention = lax.dynamic_slice_in_dim(attention_low, start, n_rows, axis=1)
    grad_query = jnp.dot(own_rows, keys_all, preferred_element_type=jnp.float32)
    grad_key = contract_first(own_cols, query_all)
    grad_value = contract_first(own_attention, grad_out_all)
    grad_heads = jnp.concatenate([grad_query, grad_key, grad_value], axis=1).astype(jnp.bfloat16)

    g_lo = grad_heads[:, :half]
    g_hi = grad_heads[:, half:]
    g_mine = jnp.where(first, g_lo, g_hi)
    g_other = jnp.where(first, g_hi, g_lo)

    input_grad = (
        contract_last(g_mine, w_mine_all) + contract_last(g_other, w_other_all)
    ).astype(jnp.bfloat16)

    blocked = features.reshape(n_rows, outer_fsdp, inner_fsdp, rows_w)
    wg_mine = jnp.einsum("pyzd,pc->zydc", blocked, g_mine, preferred_element_type=jnp.float32)
    wg_other = jnp.einsum("pyzd,pc->zydc", blocked, g_other, preferred_element_type=jnp.float32)
    wg_from_partner = dp_partner(wg_other.astype(jnp.bfloat16), 1)
    blocks = wg_mine + wg_from_partner.astype(jnp.float32)
    over_z = ring_reduce_scatter(blocks, ring_z, axis=0)
    over_fsdp = ring_reduce_scatter(over_z, ring_y)

    by_seq = lax.all_gather(over_fsdp, "seq", axis=0, tiled=False)
    over_seq = by_seq[0]
    for s_i in range(1, by_seq.shape[0]):
        over_seq = over_seq + by_seq[s_i]
    by_dp = lax.all_gather(over_seq, "dp", axis=0, tiled=False)
    halves = []
    for c in range(2):
        part = by_dp[c]
        for d in range(c + 2, by_dp.shape[0], 2):
            part = part + by_dp[d]
        halves.append(part)
    weight_grad = jnp.concatenate(halves, axis=1)
    return (input_grad[None], weight_grad)


def inner_ring_size(mesh):
    axis = mesh.axis_names.index("fsdp")
    line = mesh.devices[tuple(0 if a != axis else slice(None) for a in range(mesh.devices.ndim))]
    line = list(line)
    if not hasattr(line[0], "coords"):
        return len(line)
    count = 1
    while count < len(line) and line[count].coords[1] == line[0].coords[1]:
        count += 1
    return count


def solution(mesh):
    placed = (
        P(("dp", "fsdp"), "seq", None),
        P(("dp", "fsdp"), "seq"),
        P("fsdp", None),
        P(("dp", "fsdp"), "seq", None),
    )
    return jax.shard_map(
        functools.partial(shards, inner_fsdp=inner_ring_size(mesh)),
        mesh=mesh,
        in_specs=placed,
        out_specs=(P(("dp", "fsdp"), "seq", None), P("fsdp", None)),
        check_vma=False,
    )
```

```python
import functools

import jax
import jax.numpy as jnp
from jax import lax
from jax.sharding import PartitionSpec as P


def contract_first(left, right):
    return lax.dot_general(
        left, right, (((0,), (0,)), ((), ())), preferred_element_type=jnp.float32
    )


def contract_last(left, right):
    return lax.dot_general(
        left, right, (((1,), (1,)), ((), ())), preferred_element_type=jnp.float32
    )


def dp_partner(x, bit):
    pairs = [(i, i ^ bit) for i in range(lax.axis_size("dp"))]
    return lax.ppermute(x, "dp", perm=pairs)


class Ring:
    def __init__(self, axis, size, inner):
        self.axis, self.size, self.inner = axis, size, inner

    def total(self):
        return lax.axis_size(self.axis)

    def position(self):
        return (lax.axis_index(self.axis) // self.inner) % self.size

    def shift(self, x, step):
        n, inner, total = self.size, self.inner, self.total()
        pairs = []
        for i in range(total):
            pos = (i // inner) % n
            base = i - pos * inner
            pairs.append((i, base + ((pos + step) % n) * inner))
        return lax.ppermute(x, self.axis, perm=pairs)


def ring_gather(x, ring, beside=None):
    n = ring.size
    got, slot = [x], {0: 0}
    cw, ccw = x, x
    for t in range(1, n):
        if t % 2 == 1:
            cw = ring.shift(cw, 1)
            if t == 1 and beside is not None:
                cw, beside = lax.optimization_barrier((cw, beside))
            slot[(n - (t + 1) // 2) % n] = len(got)
            got.append(cw)
        else:
            ccw = ring.shift(ccw, -1)
            slot[t // 2] = len(got)
            got.append(ccw)
    return jnp.stack(got), [slot[k] for k in range(n)], beside


def ring_reduce_scatter(blocks, ring, axis=0, beside=None):
    n = ring.size
    me = ring.position()

    def pick(index):
        return lax.dynamic_index_in_dim(blocks, index % n, axis=axis, keepdims=False)

    total = pick(me)
    if n == 1:
        return total, beside
    up, down = n // 2, (n - 1) // 2
    acc = pick(me + up)
    for t in range(1, up + 1):
        acc = ring.shift(acc.astype(jnp.bfloat16), 1)
        if t == 1 and beside is not None:
            acc, beside = lax.optimization_barrier((acc, beside))
        acc = acc.astype(jnp.float32)
        if t < up:
            acc = acc + pick(me + up - t)
    total = total + acc
    if down:
        acc = pick(me - down)
        for t in range(1, down + 1):
            acc = ring.shift(acc.astype(jnp.bfloat16), -1).astype(jnp.float32)
            if t < down:
                acc = acc + pick(me - down + t)
        total = total + acc
    return total, beside


def shards(patches, segments, qkv_weight, cotangent, inner_fsdp):
    features = patches[0]
    image_ids = segments[0]
    grad_out = cotangent[0]
    width_head = cotangent.shape[2]
    width_all = qkv_weight.shape[1]
    rows_w = qkv_weight.shape[0]
    half = width_all // 2
    scale = width_head ** (-0.5)
    core = lax.axis_index("dp") % 2
    first = core == 0
    n_fsdp = lax.axis_size("fsdp")
    outer_fsdp = n_fsdp // inner_fsdp
    ring_y = Ring("fsdp", outer_fsdp, inner_fsdp)
    ring_z = Ring("fsdp", inner_fsdp, 1)
    ring_x = Ring("seq", lax.axis_size("seq"), 1)

    w_mine = lax.dynamic_slice_in_dim(qkv_weight, core * half, half, axis=1)
    stack_y, slot_y, _ = ring_gather(w_mine, ring_y)
    blocked = features.reshape(features.shape[0], outer_fsdp, inner_fsdp, rows_w)
    stack_zy, slot_z, blocked = ring_gather(stack_y, ring_z, beside=blocked)
    flat = stack_zy.reshape(-1, rows_w, half)
    me_y, me_z = ring_y.position(), ring_z.position()
    absolute = jnp.arange(n_fsdp, dtype=jnp.int32)
    rel_y = (absolute // inner_fsdp - me_y) % outer_fsdp
    rel_z = (absolute % inner_fsdp - me_z) % inner_fsdp
    order = jnp.asarray(slot_z, jnp.int32)[rel_z] * outer_fsdp + jnp.asarray(slot_y, jnp.int32)[rel_y]
    w_mine_all = jnp.take(flat, order, axis=0, mode="clip").reshape(n_fsdp * rows_w, half)
    w_other_all = dp_partner(w_mine_all, 1)

    h_mine = jnp.dot(features, w_mine_all, preferred_element_type=jnp.float32)
    h_other = jnp.dot(features, w_other_all, preferred_element_type=jnp.float32)
    projected = jnp.where(
        first,
        jnp.concatenate([h_mine, h_other], axis=1),
        jnp.concatenate([h_other, h_mine], axis=1),
    )
    heads = projected.astype(jnp.bfloat16)
    n_rows = features.shape[0]
    n_x = ring_x.size
    me_x = ring_x.position()
    ids_col = jnp.broadcast_to(image_ids.astype(jnp.bfloat16)[:, None], (n_rows, width_head))
    packed = jnp.concatenate([heads, grad_out, ids_col], axis=1)
    packed_all = lax.all_gather(packed, "seq", axis=0, tiled=True)
    query_all = packed_all[:, :width_head]
    keys_all = packed_all[:, width_head : 2 * width_head]
    values_all = packed_all[:, 2 * width_head : 3 * width_head]
    grad_out_all = packed_all[:, 3 * width_head : 4 * width_head]
    images_all = packed_all[:, 4 * width_head]
    scores = contract_last(query_all, keys_all) * scale
    allowed = images_all[:, None] == images_all[None, :]
    highest = jnp.max(jnp.where(allowed, scores, -jnp.inf), axis=1)
    summed = jnp.sum(jnp.where(allowed, jnp.exp(scores - highest[:, None]), 0.0), axis=1)
    log_total = highest + jnp.log(summed)
    attention = jnp.where(allowed, jnp.exp(scores - log_total[:, None]), 0.0)
    attention_low = attention.astype(jnp.bfloat16)
    output = jnp.dot(attention_low, values_all, preferred_element_type=jnp.float32)
    delta_rows = jnp.sum(grad_out_all.astype(jnp.float32) * output, axis=1)
    grad_attention = contract_last(grad_out_all, values_all)
    grad_scores = (attention * (grad_attention - delta_rows[:, None]) * scale).astype(jnp.bfloat16)
    start = me_x * n_rows
    own_rows = lax.dynamic_slice_in_dim(grad_scores, start, n_rows, axis=0)
    own_cols = lax.dynamic_slice_in_dim(grad_scores, start, n_rows, axis=1)
    own_attention = lax.dynamic_slice_in_dim(attention_low, start, n_rows, axis=1)
    grad_query = jnp.dot(own_rows, keys_all, preferred_element_type=jnp.float32)
    grad_key = contract_first(own_cols, query_all)
    grad_value = contract_first(own_attention, grad_out_all)
    grad_heads = jnp.concatenate([grad_query, grad_key, grad_value], axis=1).astype(jnp.bfloat16)

    g_lo = grad_heads[:, :half]
    g_hi = grad_heads[:, half:]
    g_mine = jnp.where(first, g_lo, g_hi)
    g_other = jnp.where(first, g_hi, g_lo)

    input_grad = (
        contract_last(g_mine, w_mine_all) + contract_last(g_other, w_other_all)
    ).astype(jnp.bfloat16)

    wg_other = jnp.einsum("pyzd,pc->zydc", blocked, g_other, preferred_element_type=jnp.float32)
    wg_from_partner = dp_partner(wg_other.astype(jnp.bfloat16), 1)
    wg_mine = jnp.einsum("pyzd,pc->zydc", blocked, g_mine, preferred_element_type=jnp.float32)
    wg_mine, wg_from_partner = lax.optimization_barrier((wg_mine, wg_from_partner))
    blocks = wg_mine + wg_from_partner.astype(jnp.float32)
    over_z, input_grad = ring_reduce_scatter(blocks, ring_z, axis=0, beside=input_grad)
    over_fsdp, _ = ring_reduce_scatter(over_z, ring_y)

    by_seq = lax.all_gather(over_fsdp, "seq", axis=0, tiled=False)
    over_seq = by_seq[0]
    for s_i in range(1, by_seq.shape[0]):
        over_seq = over_seq + by_seq[s_i]
    by_dp = lax.all_gather(over_seq, "dp", axis=0, tiled=False)
    halves = []
    for c in range(2):
        part = by_dp[c]
        for d in range(c + 2, by_dp.shape[0], 2):
            part = part + by_dp[d]
        halves.append(part)
    weight_grad = jnp.concatenate(halves, axis=1)
    return (input_grad[None], weight_grad)


def inner_ring_size(mesh):
    axis = mesh.axis_names.index("fsdp")
    line = mesh.devices[tuple(0 if a != axis else slice(None) for a in range(mesh.devices.ndim))]
    line = list(line)
    if not hasattr(line[0], "coords"):
        return len(line)
    count = 1
    while count < len(line) and line[count].coords[1] == line[0].coords[1]:
        count += 1
    return count


def solution(mesh):
    placed = (
        P(("dp", "fsdp"), "seq", None),
        P(("dp", "fsdp"), "seq"),
        P("fsdp", None),
        P(("dp", "fsdp"), "seq", None),
    )
    return jax.shard_map(
        functools.partial(shards, inner_fsdp=inner_ring_size(mesh)),
        mesh=mesh,
        in_specs=placed,
        out_specs=(P(("dp", "fsdp"), "seq", None), P("fsdp", None)),
        check_vma=False,
    )
```

```python
import functools

import jax
import jax.numpy as jnp
from jax import lax
from jax.sharding import PartitionSpec as P


def contract_first(left, right):
    return lax.dot_general(
        left, right, (((0,), (0,)), ((), ())), preferred_element_type=jnp.float32
    )


def contract_last(left, right):
    return lax.dot_general(
        left, right, (((1,), (1,)), ((), ())), preferred_element_type=jnp.float32
    )


def dp_partner(x, bit):
    pairs = [(i, i ^ bit) for i in range(lax.axis_size("dp"))]
    return lax.ppermute(x, "dp", perm=pairs)


class Ring:
    def __init__(self, axis, size, inner):
        self.axis, self.size, self.inner = axis, size, inner

    def total(self):
        return lax.axis_size(self.axis)

    def position(self):
        return (lax.axis_index(self.axis) // self.inner) % self.size

    def shift(self, x, step):
        n, inner, total = self.size, self.inner, self.total()
        pairs = []
        for i in range(total):
            pos = (i // inner) % n
            base = i - pos * inner
            pairs.append((i, base + ((pos + step) % n) * inner))
        return lax.ppermute(x, self.axis, perm=pairs)


def halves_axis(shape):
    return 0 if shape[0] % 2 == 0 else 1


def split_halves(x):
    axis = halves_axis(x.shape)
    size = x.shape[axis]
    return (
        lax.slice_in_dim(x, 0, size // 2, axis=axis),
        lax.slice_in_dim(x, size // 2, size, axis=axis),
        axis,
    )


def ring_gather(x, ring, beside=None):
    n = ring.size
    by_offset = {0: x}
    cw, ccw = x, x
    far = n // 2 if n % 2 == 0 else None
    for t in range(1, (n - 1) // 2 + 1):
        cw = ring.shift(cw, 1)
        by_offset[n - t] = cw
        ccw = ring.shift(ccw, -1)
        if t == 1 and beside is not None:
            ccw, beside = lax.optimization_barrier((ccw, beside))
        by_offset[t] = ccw
    if far is not None:
        top, _, axis = split_halves(cw)
        _, bottom, _ = split_halves(ccw)
        top = ring.shift(top, 1)
        bottom = ring.shift(bottom, -1)
        if far == 1 and beside is not None:
            bottom, beside = lax.optimization_barrier((bottom, beside))
        by_offset[far] = jnp.concatenate([top, bottom], axis=axis)
    return jnp.stack([by_offset[k] for k in range(n)]), beside


def ring_reduce_scatter(blocks, ring, axis=0, beside=None):
    n = ring.size
    me = ring.position()

    def pick(index):
        return lax.dynamic_index_in_dim(blocks, index % n, axis=axis, keepdims=False)

    def send(value, step):
        return ring.shift(value.astype(jnp.bfloat16), step)

    total = pick(me)
    if n == 1:
        return total, beside
    h = n // 2
    even = n % 2 == 0
    results = []
    for direction in (1, -1):
        steps = h if (even or direction == 1) else (n - 1) // 2
        if steps == 0:
            continue
        start = pick(me + direction * steps)
        if even:
            top, bottom, split = split_halves(start)
            start = top if direction == 1 else bottom
        acc = send(start, direction)
        if direction == 1 and beside is not None:
            acc, beside = lax.optimization_barrier((acc, beside))
        acc = acc.astype(jnp.float32)
        for t in range(2, steps + 1):
            own = pick(me + direction * (steps - t + 1))
            if even and t == 2:
                top, bottom, split = split_halves(own)
                if direction == 1:
                    own = jnp.concatenate([top + acc, bottom], axis=split)
                else:
                    own = jnp.concatenate([top, bottom + acc], axis=split)
            else:
                own = own + acc
            acc = send(own, direction).astype(jnp.float32)
        results.append(acc)
    if even and h == 1:
        total = total + jnp.concatenate(results, axis=halves_axis(total.shape))
    else:
        for r in results:
            total = total + r
    return total, beside


def shards(patches, segments, qkv_weight, cotangent, inner_fsdp):
    features = patches[0]
    image_ids = segments[0]
    grad_out = cotangent[0]
    width_head = cotangent.shape[2]
    width_all = qkv_weight.shape[1]
    rows_w = qkv_weight.shape[0]
    half = width_all // 2
    scale = width_head ** (-0.5)
    core = lax.axis_index("dp") % 2
    first = core == 0
    n_fsdp = lax.axis_size("fsdp")
    outer_fsdp = n_fsdp // inner_fsdp
    ring_y = Ring("fsdp", outer_fsdp, inner_fsdp)
    ring_z = Ring("fsdp", inner_fsdp, 1)
    ring_x = Ring("seq", lax.axis_size("seq"), 1)

    w_mine = lax.dynamic_slice_in_dim(qkv_weight, core * half, half, axis=1)
    stack_y, _ = ring_gather(w_mine, ring_y)
    blocked = features.reshape(features.shape[0], outer_fsdp, inner_fsdp, rows_w)
    stack_zy, blocked = ring_gather(stack_y, ring_z, beside=blocked)
    flat = stack_zy.reshape(-1, rows_w, half)
    me_y, me_z = ring_y.position(), ring_z.position()
    absolute = jnp.arange(n_fsdp, dtype=jnp.int32)
    rel_y = (absolute // inner_fsdp - me_y) % outer_fsdp
    rel_z = (absolute % inner_fsdp - me_z) % inner_fsdp
    order = rel_z * outer_fsdp + rel_y
    w_mine_all = jnp.take(flat, order, axis=0, mode="clip").reshape(n_fsdp * rows_w, half)
    w_other_all = dp_partner(w_mine_all, 1)

    h_mine = jnp.dot(features, w_mine_all, preferred_element_type=jnp.float32)
    h_other = jnp.dot(features, w_other_all, preferred_element_type=jnp.float32)
    projected = jnp.where(
        first,
        jnp.concatenate([h_mine, h_other], axis=1),
        jnp.concatenate([h_other, h_mine], axis=1),
    )
    heads = projected.astype(jnp.bfloat16)
    n_rows = features.shape[0]
    n_x = ring_x.size
    me_x = ring_x.position()
    ids_col = jnp.broadcast_to(image_ids.astype(jnp.bfloat16)[:, None], (n_rows, width_head))
    packed = jnp.concatenate([heads, grad_out, ids_col], axis=1)
    packed_all = lax.all_gather(packed, "seq", axis=0, tiled=True)
    query_all = packed_all[:, :width_head]
    keys_all = packed_all[:, width_head : 2 * width_head]
    values_all = packed_all[:, 2 * width_head : 3 * width_head]
    grad_out_all = packed_all[:, 3 * width_head : 4 * width_head]
    images_all = packed_all[:, 4 * width_head]
    scores = contract_last(query_all, keys_all) * scale
    allowed = images_all[:, None] == images_all[None, :]
    highest = jnp.max(jnp.where(allowed, scores, -jnp.inf), axis=1)
    summed = jnp.sum(jnp.where(allowed, jnp.exp(scores - highest[:, None]), 0.0), axis=1)
    log_total = highest + jnp.log(summed)
    attention = jnp.where(allowed, jnp.exp(scores - log_total[:, None]), 0.0)
    attention_low = attention.astype(jnp.bfloat16)
    output = jnp.dot(attention_low, values_all, preferred_element_type=jnp.float32)
    delta_rows = jnp.sum(grad_out_all.astype(jnp.float32) * output, axis=1)
    grad_attention = contract_last(grad_out_all, values_all)
    grad_scores = (attention * (grad_attention - delta_rows[:, None]) * scale).astype(jnp.bfloat16)
    start = me_x * n_rows
    own_rows = lax.dynamic_slice_in_dim(grad_scores, start, n_rows, axis=0)
    own_cols = lax.dynamic_slice_in_dim(grad_scores, start, n_rows, axis=1)
    own_attention = lax.dynamic_slice_in_dim(attention_low, start, n_rows, axis=1)
    grad_query = jnp.dot(own_rows, keys_all, preferred_element_type=jnp.float32)
    grad_key = contract_first(own_cols, query_all)
    grad_value = contract_first(own_attention, grad_out_all)
    grad_heads = jnp.concatenate([grad_query, grad_key, grad_value], axis=1).astype(jnp.bfloat16)

    g_lo = grad_heads[:, :half]
    g_hi = grad_heads[:, half:]
    g_mine = jnp.where(first, g_lo, g_hi)
    g_other = jnp.where(first, g_hi, g_lo)

    input_grad = (
        contract_last(g_mine, w_mine_all) + contract_last(g_other, w_other_all)
    ).astype(jnp.bfloat16)

    wg_other = jnp.einsum("pyzd,pc->zydc", blocked, g_other, preferred_element_type=jnp.float32)
    wg_from_partner = dp_partner(wg_other.astype(jnp.bfloat16), 1)
    wg_mine = jnp.einsum("pyzd,pc->zydc", blocked, g_mine, preferred_element_type=jnp.float32)
    wg_mine, wg_from_partner = lax.optimization_barrier((wg_mine, wg_from_partner))
    blocks = wg_mine + wg_from_partner.astype(jnp.float32)
    over_z, input_grad = ring_reduce_scatter(blocks, ring_z, axis=0, beside=input_grad)
    over_fsdp, _ = ring_reduce_scatter(over_z, ring_y)

    by_seq = lax.all_gather(over_fsdp, "seq", axis=0, tiled=False)
    over_seq = by_seq[0]
    for s_i in range(1, by_seq.shape[0]):
        over_seq = over_seq + by_seq[s_i]
    by_dp = lax.all_gather(over_seq, "dp", axis=0, tiled=False)
    halves = []
    for c in range(2):
        part = by_dp[c]
        for d in range(c + 2, by_dp.shape[0], 2):
            part = part + by_dp[d]
        halves.append(part)
    weight_grad = jnp.concatenate(halves, axis=1)
    return (input_grad[None], weight_grad)


def inner_ring_size(mesh):
    axis = mesh.axis_names.index("fsdp")
    line = mesh.devices[tuple(0 if a != axis else slice(None) for a in range(mesh.devices.ndim))]
    line = list(line)
    if not hasattr(line[0], "coords"):
        return len(line)
    count = 1
    while count < len(line) and line[count].coords[1] == line[0].coords[1]:
        count += 1
    return count


def solution(mesh):
    placed = (
        P(("dp", "fsdp"), "seq", None),
        P(("dp", "fsdp"), "seq"),
        P("fsdp", None),
        P(("dp", "fsdp"), "seq", None),
    )
    return jax.shard_map(
        functools.partial(shards, inner_fsdp=inner_ring_size(mesh)),
        mesh=mesh,
        in_specs=placed,
        out_specs=(P(("dp", "fsdp"), "seq", None), P("fsdp", None)),
        check_vma=False,
    )
```

```python
import functools

import jax
import jax.numpy as jnp
from jax import lax
from jax.sharding import PartitionSpec as P


def contract_first(left, right):
    return lax.dot_general(
        left, right, (((0,), (0,)), ((), ())), preferred_element_type=jnp.float32
    )


def contract_last(left, right):
    return lax.dot_general(
        left, right, (((1,), (1,)), ((), ())), preferred_element_type=jnp.float32
    )


def dp_partner(x, bit):
    pairs = [(i, i ^ bit) for i in range(lax.axis_size("dp"))]
    return lax.ppermute(x, "dp", perm=pairs)


class Ring:
    def __init__(self, axis, size, inner):
        self.axis, self.size, self.inner = axis, size, inner

    def total(self):
        return lax.axis_size(self.axis)

    def position(self):
        return (lax.axis_index(self.axis) // self.inner) % self.size

    def shift(self, x, step):
        n, inner, total = self.size, self.inner, self.total()
        pairs = []
        for i in range(total):
            pos = (i // inner) % n
            base = i - pos * inner
            pairs.append((i, base + ((pos + step) % n) * inner))
        return lax.ppermute(x, self.axis, perm=pairs)


def ring_gather(x, ring, beside=None):
    n = ring.size
    got, slot = [x], {0: 0}
    cw, ccw = x, x
    for t in range(1, n):
        if t % 2 == 1:
            cw = ring.shift(cw, 1)
            if t == 1 and beside is not None:
                cw, beside = lax.optimization_barrier((cw, beside))
            slot[(n - (t + 1) // 2) % n] = len(got)
            got.append(cw)
        else:
            ccw = ring.shift(ccw, -1)
            slot[t // 2] = len(got)
            got.append(ccw)
    return jnp.stack(got), [slot[k] for k in range(n)], beside


def ring_reduce_scatter(blocks, ring, axis=0, beside=None):
    n = ring.size
    me = ring.position()

    def pick(index):
        if isinstance(blocks, tuple):
            return sum(
                lax.dynamic_index_in_dim(b, index % n, axis=axis, keepdims=False).astype(jnp.float32)
                for b in blocks
            )
        return lax.dynamic_index_in_dim(blocks, index % n, axis=axis, keepdims=False)

    total = pick(me)
    if n == 1:
        return total, beside
    up, down = n // 2, (n - 1) // 2
    acc = pick(me + up)
    for t in range(1, up + 1):
        acc = ring.shift(acc.astype(jnp.bfloat16), 1)
        if t == 1 and beside is not None:
            acc, beside = lax.optimization_barrier((acc, beside))
        acc = acc.astype(jnp.float32)
        if t < up:
            acc = acc + pick(me + up - t)
    total = total + acc
    if down:
        acc = pick(me - down)
        for t in range(1, down + 1):
            acc = ring.shift(acc.astype(jnp.bfloat16), -1).astype(jnp.float32)
            if t < down:
                acc = acc + pick(me - down + t)
        total = total + acc
    return total, beside


def shards(patches, segments, qkv_weight, cotangent, inner_fsdp):
    features = patches[0]
    image_ids = segments[0]
    grad_out = cotangent[0]
    width_head = cotangent.shape[2]
    width_all = qkv_weight.shape[1]
    rows_w = qkv_weight.shape[0]
    half = width_all // 2
    scale = width_head ** (-0.5)
    core = lax.axis_index("dp") % 2
    first = core == 0
    n_fsdp = lax.axis_size("fsdp")
    outer_fsdp = n_fsdp // inner_fsdp
    ring_y = Ring("fsdp", outer_fsdp, inner_fsdp)
    ring_z = Ring("fsdp", inner_fsdp, 1)
    ring_x = Ring("seq", lax.axis_size("seq"), 1)

    w_mine = lax.dynamic_slice_in_dim(qkv_weight, core * half, half, axis=1)
    stack_y, slot_y, _ = ring_gather(w_mine, ring_y)
    blocked = features.reshape(features.shape[0], outer_fsdp, inner_fsdp, rows_w)
    stack_zy, slot_z, blocked = ring_gather(stack_y, ring_z, beside=blocked)
    flat = stack_zy.reshape(-1, rows_w, half)
    me_y, me_z = ring_y.position(), ring_z.position()
    absolute = jnp.arange(n_fsdp, dtype=jnp.int32)
    rel_y = (absolute // inner_fsdp - me_y) % outer_fsdp
    rel_z = (absolute % inner_fsdp - me_z) % inner_fsdp
    order = jnp.asarray(slot_z, jnp.int32)[rel_z] * outer_fsdp + jnp.asarray(slot_y, jnp.int32)[rel_y]
    w_mine_all = jnp.take(flat, order, axis=0, mode="clip").reshape(n_fsdp * rows_w, half)
    w_other_all = dp_partner(w_mine_all, 1)

    h_mine = jnp.dot(features, w_mine_all, preferred_element_type=jnp.float32)
    h_other = jnp.dot(features, w_other_all, preferred_element_type=jnp.float32)
    projected = jnp.where(
        first,
        jnp.concatenate([h_mine, h_other], axis=1),
        jnp.concatenate([h_other, h_mine], axis=1),
    )
    heads = projected.astype(jnp.bfloat16)
    n_rows = features.shape[0]
    n_x = ring_x.size
    me_x = ring_x.position()
    ids_col = jnp.broadcast_to(image_ids.astype(jnp.bfloat16)[:, None], (n_rows, width_head))
    packed = jnp.concatenate([heads, grad_out, ids_col], axis=1)
    packed_all = lax.all_gather(packed, "seq", axis=0, tiled=True)
    query_all = packed_all[:, :width_head]
    keys_all = packed_all[:, width_head : 2 * width_head]
    values_all = packed_all[:, 2 * width_head : 3 * width_head]
    grad_out_all = packed_all[:, 3 * width_head : 4 * width_head]
    images_all = packed_all[:, 4 * width_head]
    scores = contract_last(query_all, keys_all) * scale
    allowed = images_all[:, None] == images_all[None, :]
    highest = jnp.max(jnp.where(allowed, scores, -jnp.inf), axis=1)
    summed = jnp.sum(jnp.where(allowed, jnp.exp(scores - highest[:, None]), 0.0), axis=1)
    log_total = highest + jnp.log(summed)
    attention = jnp.where(allowed, jnp.exp(scores - log_total[:, None]), 0.0)
    attention_low = attention.astype(jnp.bfloat16)
    output = jnp.dot(attention_low, values_all, preferred_element_type=jnp.float32)
    delta_rows = jnp.sum(grad_out_all.astype(jnp.float32) * output, axis=1)
    grad_attention = contract_last(grad_out_all, values_all)
    grad_scores = (attention * (grad_attention - delta_rows[:, None]) * scale).astype(jnp.bfloat16)
    start = me_x * n_rows
    own_rows = lax.dynamic_slice_in_dim(grad_scores, start, n_rows, axis=0)
    own_cols = lax.dynamic_slice_in_dim(grad_scores, start, n_rows, axis=1)
    own_attention = lax.dynamic_slice_in_dim(attention_low, start, n_rows, axis=1)
    grad_query = jnp.dot(own_rows, keys_all, preferred_element_type=jnp.float32)
    grad_key = contract_first(own_cols, query_all)
    grad_value = contract_first(own_attention, grad_out_all)
    grad_heads = jnp.concatenate([grad_query, grad_key, grad_value], axis=1).astype(jnp.bfloat16)

    g_lo = grad_heads[:, :half]
    g_hi = grad_heads[:, half:]
    g_mine = jnp.where(first, g_lo, g_hi)
    g_other = jnp.where(first, g_hi, g_lo)

    input_grad = (
        contract_last(g_mine, w_mine_all) + contract_last(g_other, w_other_all)
    ).astype(jnp.bfloat16)

    wg_other = jnp.einsum("pyzd,pc->zydc", blocked, g_other, preferred_element_type=jnp.float32)
    wg_from_partner = dp_partner(wg_other.astype(jnp.bfloat16), 1)
    wg_mine = jnp.einsum("pyzd,pc->zydc", blocked, g_mine, preferred_element_type=jnp.float32)
    wg_mine, wg_from_partner = lax.optimization_barrier((wg_mine, wg_from_partner))
    blocks = (wg_mine, wg_from_partner)
    over_z, input_grad = ring_reduce_scatter(blocks, ring_z, axis=0, beside=input_grad)
    over_fsdp, _ = ring_reduce_scatter(over_z, ring_y)

    by_seq = lax.all_gather(over_fsdp, "seq", axis=0, tiled=False)
    over_seq = by_seq[0]
    for s_i in range(1, by_seq.shape[0]):
        over_seq = over_seq + by_seq[s_i]
    by_dp = lax.all_gather(over_seq, "dp", axis=0, tiled=False)
    halves = []
    for c in range(2):
        part = by_dp[c]
        for d in range(c + 2, by_dp.shape[0], 2):
            part = part + by_dp[d]
        halves.append(part)
    weight_grad = jnp.concatenate(halves, axis=1)
    return (input_grad[None], weight_grad)


def inner_ring_size(mesh):
    axis = mesh.axis_names.index("fsdp")
    line = mesh.devices[tuple(0 if a != axis else slice(None) for a in range(mesh.devices.ndim))]
    line = list(line)
    if not hasattr(line[0], "coords"):
        return len(line)
    count = 1
    while count < len(line) and line[count].coords[1] == line[0].coords[1]:
        count += 1
    return count


def solution(mesh):
    placed = (
        P(("dp", "fsdp"), "seq", None),
        P(("dp", "fsdp"), "seq"),
        P("fsdp", None),
        P(("dp", "fsdp"), "seq", None),
    )
    return jax.shard_map(
        functools.partial(shards, inner_fsdp=inner_ring_size(mesh)),
        mesh=mesh,
        in_specs=placed,
        out_specs=(P(("dp", "fsdp"), "seq", None), P("fsdp", None)),
        check_vma=False,
    )
```

```python
import functools

import jax
import jax.numpy as jnp
from jax import lax
from jax.sharding import PartitionSpec as P


def contract_first(left, right):
    return lax.dot_general(
        left, right, (((0,), (0,)), ((), ())), preferred_element_type=jnp.float32
    )


def contract_last(left, right):
    return lax.dot_general(
        left, right, (((1,), (1,)), ((), ())), preferred_element_type=jnp.float32
    )


def dp_partner(x, bit):
    pairs = [(i, i ^ bit) for i in range(lax.axis_size("dp"))]
    return lax.ppermute(x, "dp", perm=pairs)


class Ring:
    def __init__(self, axis, size, inner):
        self.axis, self.size, self.inner = axis, size, inner

    def total(self):
        return lax.axis_size(self.axis)

    def position(self):
        return (lax.axis_index(self.axis) // self.inner) % self.size

    def shift(self, x, step):
        n, inner, total = self.size, self.inner, self.total()
        pairs = []
        for i in range(total):
            pos = (i // inner) % n
            base = i - pos * inner
            pairs.append((i, base + ((pos + step) % n) * inner))
        return lax.ppermute(x, self.axis, perm=pairs)


def ring_gather(x, ring, beside=None):
    n = ring.size
    got, slot = [x], {0: 0}
    cw, ccw = x, x
    for t in range(1, n):
        if t % 2 == 1:
            cw = ring.shift(cw, 1)
            if t == 1 and beside is not None:
                cw, beside = lax.optimization_barrier((cw, beside))
            slot[(n - (t + 1) // 2) % n] = len(got)
            got.append(cw)
        else:
            ccw = ring.shift(ccw, -1)
            slot[t // 2] = len(got)
            got.append(ccw)
    return jnp.stack(got), [slot[k] for k in range(n)], beside


def ring_reduce_scatter(blocks, ring, axis=0, beside=None):
    n = ring.size
    me = ring.position()

    def pick(index):
        return lax.dynamic_index_in_dim(blocks, index % n, axis=axis, keepdims=False)

    total = pick(me)
    if n == 1:
        return total, beside
    up, down = n // 2, (n - 1) // 2
    acc = pick(me + up)
    for t in range(1, up + 1):
        acc = ring.shift(acc.astype(jnp.bfloat16), 1)
        if t == 1 and beside is not None:
            acc, beside = lax.optimization_barrier((acc, beside))
        acc = acc.astype(jnp.float32)
        if t < up:
            acc = acc + pick(me + up - t)
    total = total + acc
    if down:
        acc = pick(me - down)
        for t in range(1, down + 1):
            acc = ring.shift(acc.astype(jnp.bfloat16), -1).astype(jnp.float32)
            if t < down:
                acc = acc + pick(me - down + t)
        total = total + acc
    return total, beside


def shards(patches, segments, qkv_weight, cotangent, inner_fsdp):
    features = patches[0]
    image_ids = segments[0]
    grad_out = cotangent[0]
    width_head = cotangent.shape[2]
    width_all = qkv_weight.shape[1]
    rows_w = qkv_weight.shape[0]
    half = width_all // 2
    scale = width_head ** (-0.5)
    core = lax.axis_index("dp") % 2
    first = core == 0
    outer_fsdp = lax.axis_size("fh")
    n_fsdp = outer_fsdp * inner_fsdp
    ring_y = Ring("fh", outer_fsdp, 1)
    ring_z = Ring("fz", inner_fsdp, 1)
    ring_x = Ring("seq", lax.axis_size("seq"), 1)

    w_mine = lax.dynamic_slice_in_dim(qkv_weight, core * half, half, axis=1)
    stack_y = lax.all_gather(w_mine, "fh", axis=0, tiled=False)
    blocked = features.reshape(features.shape[0], outer_fsdp, inner_fsdp, rows_w)
    stack_zy, slot_z, blocked = ring_gather(stack_y, ring_z, beside=blocked)
    flat = stack_zy.reshape(-1, rows_w, half)
    me_y, me_z = ring_y.position(), ring_z.position()
    absolute = jnp.arange(n_fsdp, dtype=jnp.int32)
    rel_z = (absolute % inner_fsdp - me_z) % inner_fsdp
    order = jnp.asarray(slot_z, jnp.int32)[rel_z] * outer_fsdp + absolute // inner_fsdp
    w_mine_all = jnp.take(flat, order, axis=0, mode="clip").reshape(n_fsdp * rows_w, half)
    w_other_all = dp_partner(w_mine_all, 1)

    h_mine = jnp.dot(features, w_mine_all, preferred_element_type=jnp.float32)
    h_other = jnp.dot(features, w_other_all, preferred_element_type=jnp.float32)
    projected = jnp.where(
        first,
        jnp.concatenate([h_mine, h_other], axis=1),
        jnp.concatenate([h_other, h_mine], axis=1),
    )
    heads = projected.astype(jnp.bfloat16)
    n_rows = features.shape[0]
    n_x = ring_x.size
    me_x = ring_x.position()
    ids_col = jnp.broadcast_to(image_ids.astype(jnp.bfloat16)[:, None], (n_rows, width_head))
    packed = jnp.concatenate([heads, grad_out, ids_col], axis=1)
    packed_all = lax.all_gather(packed, "seq", axis=0, tiled=True)
    query_all = packed_all[:, :width_head]
    keys_all = packed_all[:, width_head : 2 * width_head]
    values_all = packed_all[:, 2 * width_head : 3 * width_head]
    grad_out_all = packed_all[:, 3 * width_head : 4 * width_head]
    images_all = packed_all[:, 4 * width_head]
    scores = contract_last(query_all, keys_all) * scale
    allowed = images_all[:, None] == images_all[None, :]
    highest = jnp.max(jnp.where(allowed, scores, -jnp.inf), axis=1)
    summed = jnp.sum(jnp.where(allowed, jnp.exp(scores - highest[:, None]), 0.0), axis=1)
    log_total = highest + jnp.log(summed)
    attention = jnp.where(allowed, jnp.exp(scores - log_total[:, None]), 0.0)
    attention_low = attention.astype(jnp.bfloat16)
    output = jnp.dot(attention_low, values_all, preferred_element_type=jnp.float32)
    delta_rows = jnp.sum(grad_out_all.astype(jnp.float32) * output, axis=1)
    grad_attention = contract_last(grad_out_all, values_all)
    grad_scores = (attention * (grad_attention - delta_rows[:, None]) * scale).astype(jnp.bfloat16)
    start = me_x * n_rows
    own_rows = lax.dynamic_slice_in_dim(grad_scores, start, n_rows, axis=0)
    own_cols = lax.dynamic_slice_in_dim(grad_scores, start, n_rows, axis=1)
    own_attention = lax.dynamic_slice_in_dim(attention_low, start, n_rows, axis=1)
    grad_query = jnp.dot(own_rows, keys_all, preferred_element_type=jnp.float32)
    grad_key = contract_first(own_cols, query_all)
    grad_value = contract_first(own_attention, grad_out_all)
    grad_heads = jnp.concatenate([grad_query, grad_key, grad_value], axis=1).astype(jnp.bfloat16)

    g_lo = grad_heads[:, :half]
    g_hi = grad_heads[:, half:]
    g_mine = jnp.where(first, g_lo, g_hi)
    g_other = jnp.where(first, g_hi, g_lo)

    input_grad = (
        contract_last(g_mine, w_mine_all) + contract_last(g_other, w_other_all)
    ).astype(jnp.bfloat16)

    wg_other = jnp.einsum("pyzd,pc->zydc", blocked, g_other, preferred_element_type=jnp.float32)
    wg_from_partner = dp_partner(wg_other.astype(jnp.bfloat16), 1)
    wg_mine = jnp.einsum("pyzd,pc->zydc", blocked, g_mine, preferred_element_type=jnp.float32)
    wg_mine, wg_from_partner = lax.optimization_barrier((wg_mine, wg_from_partner))
    blocks = wg_mine + wg_from_partner.astype(jnp.float32)
    over_z, input_grad = ring_reduce_scatter(blocks, ring_z, axis=0, beside=input_grad)
    over_fsdp, _ = ring_reduce_scatter(over_z, ring_y)

    by_seq = lax.all_gather(over_fsdp, "seq", axis=0, tiled=False)
    over_seq = by_seq[0]
    for s_i in range(1, by_seq.shape[0]):
        over_seq = over_seq + by_seq[s_i]
    by_dp = lax.all_gather(over_seq, "dp", axis=0, tiled=False)
    halves = []
    for c in range(2):
        part = by_dp[c]
        for d in range(c + 2, by_dp.shape[0], 2):
            part = part + by_dp[d]
        halves.append(part)
    weight_grad = jnp.concatenate(halves, axis=1)
    return (input_grad[None], weight_grad)


def inner_ring_size(mesh):
    axis = mesh.axis_names.index("fsdp")
    line = mesh.devices[tuple(0 if a != axis else slice(None) for a in range(mesh.devices.ndim))]
    line = list(line)
    if not hasattr(line[0], "coords"):
        return len(line)
    count = 1
    while count < len(line) and line[count].coords[1] == line[0].coords[1]:
        count += 1
    return count


def solution(mesh):
    inner = inner_ring_size(mesh)
    sizes = dict(zip(mesh.axis_names, mesh.devices.shape))
    split = jax.sharding.Mesh(
        mesh.devices.reshape(sizes["dp"], sizes["seq"], sizes["fsdp"] // inner, inner),
        ("dp", "seq", "fh", "fz"),
    )
    rows = ("dp", "fh", "fz")
    placed = (
        P(rows, "seq", None),
        P(rows, "seq"),
        P(("fh", "fz"), None),
        P(rows, "seq", None),
    )
    return jax.shard_map(
        functools.partial(shards, inner_fsdp=inner),
        mesh=split,
        in_specs=placed,
        out_specs=(P(rows, "seq", None), P(("fh", "fz"), None)),
        check_vma=False,
    )
```

```python
import functools

import jax
import jax.numpy as jnp
from jax import lax
from jax.sharding import PartitionSpec as P


def contract_first(left, right):
    return lax.dot_general(
        left, right, (((0,), (0,)), ((), ())), preferred_element_type=jnp.float32
    )


def contract_last(left, right):
    return lax.dot_general(
        left, right, (((1,), (1,)), ((), ())), preferred_element_type=jnp.float32
    )


def dp_partner(x, bit):
    pairs = [(i, i ^ bit) for i in range(lax.axis_size("dp"))]
    return lax.ppermute(x, "dp", perm=pairs)


class Ring:
    def __init__(self, axis, size, inner):
        self.axis, self.size, self.inner = axis, size, inner

    def total(self):
        return lax.axis_size(self.axis)

    def position(self):
        return (lax.axis_index(self.axis) // self.inner) % self.size

    def shift(self, x, step):
        n, inner, total = self.size, self.inner, self.total()
        pairs = []
        for i in range(total):
            pos = (i // inner) % n
            base = i - pos * inner
            pairs.append((i, base + ((pos + step) % n) * inner))
        return lax.ppermute(x, self.axis, perm=pairs)


def ring_gather(x, ring, beside=None):
    n = ring.size
    got, slot = [x], {0: 0}
    cw, ccw = x, x
    last_cw = n - 1 if (n - 1) % 2 == 1 else n - 2
    for t in range(1, n):
        if t % 2 == 1:
            cw = ring.shift(cw, 1)
            if t == last_cw and beside is not None:
                cw, beside = lax.optimization_barrier((cw, beside))
            slot[(n - (t + 1) // 2) % n] = len(got)
            got.append(cw)
        else:
            ccw = ring.shift(ccw, -1)
            slot[t // 2] = len(got)
            got.append(ccw)
    return jnp.stack(got), [slot[k] for k in range(n)], beside


def ring_reduce_scatter(blocks, ring, axis=0, beside=None):
    n = ring.size
    me = ring.position()

    def pick(index):
        return lax.dynamic_index_in_dim(blocks, index % n, axis=axis, keepdims=False)

    total = pick(me)
    if n == 1:
        return total, beside
    up, down = n // 2, (n - 1) // 2
    acc = pick(me + up)
    for t in range(1, up + 1):
        acc = ring.shift(acc.astype(jnp.bfloat16), 1)
        if t == up and beside is not None:
            acc, beside = lax.optimization_barrier((acc, beside))
        acc = acc.astype(jnp.float32)
        if t < up:
            acc = acc + pick(me + up - t)
    total = total + acc
    if down:
        acc = pick(me - down)
        for t in range(1, down + 1):
            acc = ring.shift(acc.astype(jnp.bfloat16), -1).astype(jnp.float32)
            if t < down:
                acc = acc + pick(me - down + t)
        total = total + acc
    return total, beside


def shards(patches, segments, qkv_weight, cotangent, inner_fsdp):
    features = patches[0]
    image_ids = segments[0]
    grad_out = cotangent[0]
    width_head = cotangent.shape[2]
    width_all = qkv_weight.shape[1]
    rows_w = qkv_weight.shape[0]
    half = width_all // 2
    scale = width_head ** (-0.5)
    core = lax.axis_index("dp") % 2
    first = core == 0
    outer_fsdp = lax.axis_size("fh")
    n_fsdp = outer_fsdp * inner_fsdp
    ring_y = Ring("fh", outer_fsdp, 1)
    ring_z = Ring("fz", inner_fsdp, 1)
    ring_x = Ring("seq", lax.axis_size("seq"), 1)

    w_mine = lax.dynamic_slice_in_dim(qkv_weight, core * half, half, axis=1)
    stack_y = lax.all_gather(w_mine, "fh", axis=0, tiled=False)
    blocked = features.reshape(features.shape[0], outer_fsdp, inner_fsdp, rows_w)
    stack_zy, slot_z, blocked = ring_gather(stack_y, ring_z, beside=blocked)
    flat = stack_zy.reshape(-1, rows_w, half)
    me_y, me_z = ring_y.position(), ring_z.position()
    absolute = jnp.arange(n_fsdp, dtype=jnp.int32)
    rel_z = (absolute % inner_fsdp - me_z) % inner_fsdp
    order = jnp.asarray(slot_z, jnp.int32)[rel_z] * outer_fsdp + absolute // inner_fsdp
    w_mine_all = jnp.take(flat, order, axis=0, mode="clip").reshape(n_fsdp * rows_w, half)
    w_other_all = dp_partner(w_mine_all, 1)

    h_mine = jnp.dot(features, w_mine_all, preferred_element_type=jnp.float32)
    h_other = jnp.dot(features, w_other_all, preferred_element_type=jnp.float32)
    projected = jnp.where(
        first,
        jnp.concatenate([h_mine, h_other], axis=1),
        jnp.concatenate([h_other, h_mine], axis=1),
    )
    heads = projected.astype(jnp.bfloat16)
    n_rows = features.shape[0]
    n_x = ring_x.size
    me_x = ring_x.position()
    ids_col = jnp.broadcast_to(image_ids.astype(jnp.bfloat16)[:, None], (n_rows, width_head))
    packed = jnp.concatenate([heads, grad_out, ids_col], axis=1)
    packed_all = lax.all_gather(packed, "seq", axis=0, tiled=True)
    query_all = packed_all[:, :width_head]
    keys_all = packed_all[:, width_head : 2 * width_head]
    values_all = packed_all[:, 2 * width_head : 3 * width_head]
    grad_out_all = packed_all[:, 3 * width_head : 4 * width_head]
    images_all = packed_all[:, 4 * width_head]
    scores = contract_last(query_all, keys_all) * scale
    allowed = images_all[:, None] == images_all[None, :]
    highest = jnp.max(jnp.where(allowed, scores, -jnp.inf), axis=1)
    summed = jnp.sum(jnp.where(allowed, jnp.exp(scores - highest[:, None]), 0.0), axis=1)
    log_total = highest + jnp.log(summed)
    attention = jnp.where(allowed, jnp.exp(scores - log_total[:, None]), 0.0)
    attention_low = attention.astype(jnp.bfloat16)
    output = jnp.dot(attention_low, values_all, preferred_element_type=jnp.float32)
    delta_rows = jnp.sum(grad_out_all.astype(jnp.float32) * output, axis=1)
    grad_attention = contract_last(grad_out_all, values_all)
    grad_scores = (attention * (grad_attention - delta_rows[:, None]) * scale).astype(jnp.bfloat16)
    start = me_x * n_rows
    own_rows = lax.dynamic_slice_in_dim(grad_scores, start, n_rows, axis=0)
    own_cols = lax.dynamic_slice_in_dim(grad_scores, start, n_rows, axis=1)
    own_attention = lax.dynamic_slice_in_dim(attention_low, start, n_rows, axis=1)
    grad_query = jnp.dot(own_rows, keys_all, preferred_element_type=jnp.float32)
    grad_key = contract_first(own_cols, query_all)
    grad_value = contract_first(own_attention, grad_out_all)
    grad_heads = jnp.concatenate([grad_query, grad_key, grad_value], axis=1).astype(jnp.bfloat16)

    g_lo = grad_heads[:, :half]
    g_hi = grad_heads[:, half:]
    g_mine = jnp.where(first, g_lo, g_hi)
    g_other = jnp.where(first, g_hi, g_lo)

    input_grad = (
        contract_last(g_mine, w_mine_all) + contract_last(g_other, w_other_all)
    ).astype(jnp.bfloat16)

    wg_other = jnp.einsum("pyzd,pc->zydc", blocked, g_other, preferred_element_type=jnp.float32)
    wg_from_partner = dp_partner(wg_other.astype(jnp.bfloat16), 1)
    wg_mine = jnp.einsum("pyzd,pc->zydc", blocked, g_mine, preferred_element_type=jnp.float32)
    wg_mine, wg_from_partner = lax.optimization_barrier((wg_mine, wg_from_partner))
    blocks = wg_mine + wg_from_partner.astype(jnp.float32)
    over_z, input_grad = ring_reduce_scatter(blocks, ring_z, axis=0, beside=input_grad)
    over_fsdp, _ = ring_reduce_scatter(over_z, ring_y)

    by_seq = lax.all_gather(over_fsdp, "seq", axis=0, tiled=False)
    over_seq = by_seq[0]
    for s_i in range(1, by_seq.shape[0]):
        over_seq = over_seq + by_seq[s_i]
    by_dp = lax.all_gather(over_seq, "dp", axis=0, tiled=False)
    halves = []
    for c in range(2):
        part = by_dp[c]
        for d in range(c + 2, by_dp.shape[0], 2):
            part = part + by_dp[d]
        halves.append(part)
    weight_grad = jnp.concatenate(halves, axis=1)
    return (input_grad[None], weight_grad)


def inner_ring_size(mesh):
    axis = mesh.axis_names.index("fsdp")
    line = mesh.devices[tuple(0 if a != axis else slice(None) for a in range(mesh.devices.ndim))]
    line = list(line)
    if not hasattr(line[0], "coords"):
        return len(line)
    count = 1
    while count < len(line) and line[count].coords[1] == line[0].coords[1]:
        count += 1
    return count


def solution(mesh):
    inner = inner_ring_size(mesh)
    sizes = dict(zip(mesh.axis_names, mesh.devices.shape))
    split = jax.sharding.Mesh(
        mesh.devices.reshape(sizes["dp"], sizes["seq"], sizes["fsdp"] // inner, inner),
        ("dp", "seq", "fh", "fz"),
    )
    rows = ("dp", "fh", "fz")
    placed = (
        P(rows, "seq", None),
        P(rows, "seq"),
        P(("fh", "fz"), None),
        P(rows, "seq", None),
    )
    return jax.shard_map(
        functools.partial(shards, inner_fsdp=inner),
        mesh=split,
        in_specs=placed,
        out_specs=(P(rows, "seq", None), P(("fh", "fz"), None)),
        check_vma=False,
    )
```

```python
import functools

import jax
import jax.numpy as jnp
from jax import lax
from jax.sharding import PartitionSpec as P


def contract_first(left, right):
    return lax.dot_general(
        left, right, (((0,), (0,)), ((), ())), preferred_element_type=jnp.float32
    )


def contract_last(left, right):
    return lax.dot_general(
        left, right, (((1,), (1,)), ((), ())), preferred_element_type=jnp.float32
    )


def dp_partner(x, bit):
    pairs = [(i, i ^ bit) for i in range(lax.axis_size("dp"))]
    return lax.ppermute(x, "dp", perm=pairs)


class Ring:
    def __init__(self, axis, size, inner):
        self.axis, self.size, self.inner = axis, size, inner

    def total(self):
        return lax.axis_size(self.axis)

    def position(self):
        return (lax.axis_index(self.axis) // self.inner) % self.size

    def shift(self, x, step):
        n, inner, total = self.size, self.inner, self.total()
        pairs = []
        for i in range(total):
            pos = (i // inner) % n
            base = i - pos * inner
            pairs.append((i, base + ((pos + step) % n) * inner))
        return lax.ppermute(x, self.axis, perm=pairs)


def ring_gather(x, ring, beside=None, late=None):
    n = ring.size
    got, slot = [x], {0: 0}
    cw, ccw = x, x
    last_cw = n - 1 if (n - 1) % 2 == 1 else n - 2
    last_ccw = n - 1 if (n - 1) % 2 == 0 else n - 2
    for t in range(1, n):
        if t % 2 == 1:
            cw = ring.shift(cw, 1)
            if t == 1 and beside is not None:
                cw, beside = lax.optimization_barrier((cw, beside))
            if t == last_cw and late is not None:
                cw, late = lax.optimization_barrier((cw, late))
            slot[(n - (t + 1) // 2) % n] = len(got)
            got.append(cw)
        else:
            ccw = ring.shift(ccw, -1)
            if t == last_ccw and late is not None:
                value, make = late
                ccw, value = lax.optimization_barrier((ccw, value))
                late = make(value)
            slot[t // 2] = len(got)
            got.append(ccw)
    if late is not None:
        return jnp.stack(got), [slot[k] for k in range(n)], late
    return jnp.stack(got), [slot[k] for k in range(n)], beside


def ring_reduce_scatter(blocks, ring, axis=0, beside=None):
    n = ring.size
    me = ring.position()

    def pick(index):
        return lax.dynamic_index_in_dim(blocks, index % n, axis=axis, keepdims=False)

    total = pick(me)
    if n == 1:
        return total, beside
    up, down = n // 2, (n - 1) // 2
    acc = pick(me + up)
    for t in range(1, up + 1):
        acc = ring.shift(acc.astype(jnp.bfloat16), 1)
        if t == 1 and beside is not None:
            acc, beside = lax.optimization_barrier((acc, beside))
        acc = acc.astype(jnp.float32)
        if t < up:
            acc = acc + pick(me + up - t)
    total = total + acc
    if down:
        acc = pick(me - down)
        for t in range(1, down + 1):
            acc = ring.shift(acc.astype(jnp.bfloat16), -1).astype(jnp.float32)
            if t < down:
                acc = acc + pick(me - down + t)
        total = total + acc
    return total, beside


def shards(patches, segments, qkv_weight, cotangent, inner_fsdp):
    features = patches[0]
    image_ids = segments[0]
    grad_out = cotangent[0]
    width_head = cotangent.shape[2]
    width_all = qkv_weight.shape[1]
    rows_w = qkv_weight.shape[0]
    half = width_all // 2
    scale = width_head ** (-0.5)
    core = lax.axis_index("dp") % 2
    first = core == 0
    outer_fsdp = lax.axis_size("fh")
    n_fsdp = outer_fsdp * inner_fsdp
    ring_y = Ring("fh", outer_fsdp, 1)
    ring_z = Ring("fz", inner_fsdp, 1)
    ring_x = Ring("seq", lax.axis_size("seq"), 1)

    w_mine = lax.dynamic_slice_in_dim(qkv_weight, core * half, half, axis=1)
    stack_y = lax.all_gather(w_mine, "fh", axis=0, tiled=False)
    relayout = lambda f: f.reshape(f.shape[0], outer_fsdp, inner_fsdp, rows_w)
    stack_zy, slot_z, blocked = ring_gather(stack_y, ring_z, late=(features, relayout))
    flat = stack_zy.reshape(-1, rows_w, half)
    me_y, me_z = ring_y.position(), ring_z.position()
    absolute = jnp.arange(n_fsdp, dtype=jnp.int32)
    rel_z = (absolute % inner_fsdp - me_z) % inner_fsdp
    order = jnp.asarray(slot_z, jnp.int32)[rel_z] * outer_fsdp + absolute // inner_fsdp
    w_mine_all = jnp.take(flat, order, axis=0, mode="clip").reshape(n_fsdp * rows_w, half)
    w_other_all = dp_partner(w_mine_all, 1)

    h_mine = jnp.dot(features, w_mine_all, preferred_element_type=jnp.float32)
    h_other = jnp.dot(features, w_other_all, preferred_element_type=jnp.float32)
    projected = jnp.where(
        first,
        jnp.concatenate([h_mine, h_other], axis=1),
        jnp.concatenate([h_other, h_mine], axis=1),
    )
    heads = projected.astype(jnp.bfloat16)
    n_rows = features.shape[0]
    n_x = ring_x.size
    me_x = ring_x.position()
    ids_col = jnp.broadcast_to(image_ids.astype(jnp.bfloat16)[:, None], (n_rows, width_head))
    packed = jnp.concatenate([heads, grad_out, ids_col], axis=1)
    packed_all = lax.all_gather(packed, "seq", axis=0, tiled=True)
    query_all = packed_all[:, :width_head]
    keys_all = packed_all[:, width_head : 2 * width_head]
    values_all = packed_all[:, 2 * width_head : 3 * width_head]
    grad_out_all = packed_all[:, 3 * width_head : 4 * width_head]
    images_all = packed_all[:, 4 * width_head]
    scores = contract_last(query_all, keys_all) * scale
    allowed = images_all[:, None] == images_all[None, :]
    highest = jnp.max(jnp.where(allowed, scores, -jnp.inf), axis=1)
    summed = jnp.sum(jnp.where(allowed, jnp.exp(scores - highest[:, None]), 0.0), axis=1)
    log_total = highest + jnp.log(summed)
    attention = jnp.where(allowed, jnp.exp(scores - log_total[:, None]), 0.0)
    attention_low = attention.astype(jnp.bfloat16)
    output = jnp.dot(attention_low, values_all, preferred_element_type=jnp.float32)
    delta_rows = jnp.sum(grad_out_all.astype(jnp.float32) * output, axis=1)
    grad_attention = contract_last(grad_out_all, values_all)
    grad_scores = (attention * (grad_attention - delta_rows[:, None]) * scale).astype(jnp.bfloat16)
    start = me_x * n_rows
    own_rows = lax.dynamic_slice_in_dim(grad_scores, start, n_rows, axis=0)
    own_cols = lax.dynamic_slice_in_dim(grad_scores, start, n_rows, axis=1)
    own_attention = lax.dynamic_slice_in_dim(attention_low, start, n_rows, axis=1)
    grad_query = jnp.dot(own_rows, keys_all, preferred_element_type=jnp.float32)
    grad_key = contract_first(own_cols, query_all)
    grad_value = contract_first(own_attention, grad_out_all)
    grad_heads = jnp.concatenate([grad_query, grad_key, grad_value], axis=1).astype(jnp.bfloat16)

    g_lo = grad_heads[:, :half]
    g_hi = grad_heads[:, half:]
    g_mine = jnp.where(first, g_lo, g_hi)
    g_other = jnp.where(first, g_hi, g_lo)

    input_grad = (
        contract_last(g_mine, w_mine_all) + contract_last(g_other, w_other_all)
    ).astype(jnp.bfloat16)

    wg_other = jnp.einsum("pyzd,pc->zydc", blocked, g_other, preferred_element_type=jnp.float32)
    wg_from_partner = dp_partner(wg_other.astype(jnp.bfloat16), 1)
    wg_mine = jnp.einsum("pyzd,pc->zydc", blocked, g_mine, preferred_element_type=jnp.float32)
    wg_mine, wg_from_partner = lax.optimization_barrier((wg_mine, wg_from_partner))
    blocks = wg_mine + wg_from_partner.astype(jnp.float32)
    over_z, input_grad = ring_reduce_scatter(blocks, ring_z, axis=0, beside=input_grad)
    over_fsdp, _ = ring_reduce_scatter(over_z, ring_y)

    by_seq = lax.all_gather(over_fsdp, "seq", axis=0, tiled=False)
    over_seq = by_seq[0]
    for s_i in range(1, by_seq.shape[0]):
        over_seq = over_seq + by_seq[s_i]
    by_dp = lax.all_gather(over_seq, "dp", axis=0, tiled=False)
    halves = []
    for c in range(2):
        part = by_dp[c]
        for d in range(c + 2, by_dp.shape[0], 2):
            part = part + by_dp[d]
        halves.append(part)
    weight_grad = jnp.concatenate(halves, axis=1)
    return (input_grad[None], weight_grad)


def inner_ring_size(mesh):
    axis = mesh.axis_names.index("fsdp")
    line = mesh.devices[tuple(0 if a != axis else slice(None) for a in range(mesh.devices.ndim))]
    line = list(line)
    if not hasattr(line[0], "coords"):
        return len(line)
    count = 1
    while count < len(line) and line[count].coords[1] == line[0].coords[1]:
        count += 1
    return count


def solution(mesh):
    inner = inner_ring_size(mesh)
    sizes = dict(zip(mesh.axis_names, mesh.devices.shape))
    split = jax.sharding.Mesh(
        mesh.devices.reshape(sizes["dp"], sizes["seq"], sizes["fsdp"] // inner, inner),
        ("dp", "seq", "fh", "fz"),
    )
    rows = ("dp", "fh", "fz")
    placed = (
        P(rows, "seq", None),
        P(rows, "seq"),
        P(("fh", "fz"), None),
        P(rows, "seq", None),
    )
    return jax.shard_map(
        functools.partial(shards, inner_fsdp=inner),
        mesh=split,
        in_specs=placed,
        out_specs=(P(rows, "seq", None), P(("fh", "fz"), None)),
        check_vma=False,
    )
```

```python
import functools

import jax
import jax.numpy as jnp
from jax import lax
from jax.sharding import PartitionSpec as P


def contract_first(left, right):
    return lax.dot_general(
        left, right, (((0,), (0,)), ((), ())), preferred_element_type=jnp.float32
    )


def contract_last(left, right):
    return lax.dot_general(
        left, right, (((1,), (1,)), ((), ())), preferred_element_type=jnp.float32
    )


def dp_partner(x, bit):
    pairs = [(i, i ^ bit) for i in range(lax.axis_size("dp"))]
    return lax.ppermute(x, "dp", perm=pairs)


class Ring:
    def __init__(self, axis, size, inner):
        self.axis, self.size, self.inner = axis, size, inner

    def total(self):
        return lax.axis_size(self.axis)

    def position(self):
        return (lax.axis_index(self.axis) // self.inner) % self.size

    def shift(self, x, step):
        n, inner, total = self.size, self.inner, self.total()
        pairs = []
        for i in range(total):
            pos = (i // inner) % n
            base = i - pos * inner
            pairs.append((i, base + ((pos + step) % n) * inner))
        return lax.ppermute(x, self.axis, perm=pairs)


def ring_gather(x, ring, beside=None, late=None):
    n = ring.size
    got, slot = [x], {0: 0}
    cw, ccw = x, x
    last_cw = n - 1 if (n - 1) % 2 == 1 else n - 2
    last_ccw = n - 1 if (n - 1) % 2 == 0 else n - 2
    for t in range(1, n):
        if t % 2 == 1:
            cw = ring.shift(cw, 1)
            if t == 1 and beside is not None:
                cw, beside = lax.optimization_barrier((cw, beside))
            if t == last_cw and late is not None:
                cw, late = lax.optimization_barrier((cw, late))
            slot[(n - (t + 1) // 2) % n] = len(got)
            got.append(cw)
        else:
            ccw = ring.shift(ccw, -1)
            if t == last_ccw and late is not None:
                value, make = late
                ccw, value = lax.optimization_barrier((ccw, value))
                late = make(value)
            slot[t // 2] = len(got)
            got.append(ccw)
    if late is not None:
        return jnp.stack(got), [slot[k] for k in range(n)], late
    return jnp.stack(got), [slot[k] for k in range(n)], beside


def ring_reduce_scatter(blocks, ring, axis=0, beside=None):
    n = ring.size
    me = ring.position()

    def pick(index):
        return lax.dynamic_index_in_dim(blocks, index % n, axis=axis, keepdims=False)

    total = pick(me)
    if n == 1:
        return total, (None if beside is None else beside[1](beside[0]))
    up, down = n // 2, (n - 1) // 2
    cw = pick(me + up)
    ccw = pick(me - down) if down else None
    for t in range(1, up + 1):
        cw = ring.shift(cw.astype(jnp.bfloat16), 1)
        if t == up and beside is not None and not callable(beside[1]):
            cw, beside = lax.optimization_barrier((cw, beside))
        cw = cw.astype(jnp.float32)
        if t < up:
            cw = cw + pick(me + up - t)
        if t <= down:
            ccw = ring.shift(ccw.astype(jnp.bfloat16), -1)
            if t == down and beside is not None:
                value, make = beside
                ccw, value = lax.optimization_barrier((ccw, value))
                beside = (make(value), None)
            ccw = ccw.astype(jnp.float32)
            if t < down:
                ccw = ccw + pick(me - down + t)
    total = total + cw
    if down:
        total = total + ccw
    if beside is not None:
        beside = beside[0] if beside[1] is None else beside[1](beside[0])
    return total, beside


def shards(patches, segments, qkv_weight, cotangent, inner_fsdp):
    features = patches[0]
    image_ids = segments[0]
    grad_out = cotangent[0]
    width_head = cotangent.shape[2]
    width_all = qkv_weight.shape[1]
    rows_w = qkv_weight.shape[0]
    half = width_all // 2
    scale = width_head ** (-0.5)
    core = lax.axis_index("dp") % 2
    first = core == 0
    outer_fsdp = lax.axis_size("fh")
    n_fsdp = outer_fsdp * inner_fsdp
    ring_y = Ring("fh", outer_fsdp, 1)
    ring_z = Ring("fz", inner_fsdp, 1)
    ring_x = Ring("seq", lax.axis_size("seq"), 1)

    w_mine = lax.dynamic_slice_in_dim(qkv_weight, core * half, half, axis=1)
    stack_y = lax.all_gather(w_mine, "fh", axis=0, tiled=False)
    relayout = lambda f: f.reshape(f.shape[0], outer_fsdp, inner_fsdp, rows_w)
    stack_zy, slot_z, blocked = ring_gather(stack_y, ring_z, late=(features, relayout))
    flat = stack_zy.reshape(-1, rows_w, half)
    me_y, me_z = ring_y.position(), ring_z.position()
    absolute = jnp.arange(n_fsdp, dtype=jnp.int32)
    rel_z = (absolute % inner_fsdp - me_z) % inner_fsdp
    order = jnp.asarray(slot_z, jnp.int32)[rel_z] * outer_fsdp + absolute // inner_fsdp
    w_mine_all = jnp.take(flat, order, axis=0, mode="clip").reshape(n_fsdp * rows_w, half)
    w_other_all = dp_partner(w_mine_all, 1)

    h_mine = jnp.dot(features, w_mine_all, preferred_element_type=jnp.float32)
    h_other = jnp.dot(features, w_other_all, preferred_element_type=jnp.float32)
    projected = jnp.where(
        first,
        jnp.concatenate([h_mine, h_other], axis=1),
        jnp.concatenate([h_other, h_mine], axis=1),
    )
    heads = projected.astype(jnp.bfloat16)
    n_rows = features.shape[0]
    n_x = ring_x.size
    me_x = ring_x.position()
    ids_col = jnp.broadcast_to(image_ids.astype(jnp.bfloat16)[:, None], (n_rows, width_head))
    packed = jnp.concatenate([heads, grad_out, ids_col], axis=1)
    packed_all = lax.all_gather(packed, "seq", axis=0, tiled=True)
    query_all = packed_all[:, :width_head]
    keys_all = packed_all[:, width_head : 2 * width_head]
    values_all = packed_all[:, 2 * width_head : 3 * width_head]
    grad_out_all = packed_all[:, 3 * width_head : 4 * width_head]
    images_all = packed_all[:, 4 * width_head]
    scores = contract_last(query_all, keys_all) * scale
    allowed = images_all[:, None] == images_all[None, :]
    highest = jnp.max(jnp.where(allowed, scores, -jnp.inf), axis=1)
    summed = jnp.sum(jnp.where(allowed, jnp.exp(scores - highest[:, None]), 0.0), axis=1)
    log_total = highest + jnp.log(summed)
    attention = jnp.where(allowed, jnp.exp(scores - log_total[:, None]), 0.0)
    attention_low = attention.astype(jnp.bfloat16)
    output = jnp.dot(attention_low, values_all, preferred_element_type=jnp.float32)
    delta_rows = jnp.sum(grad_out_all.astype(jnp.float32) * output, axis=1)
    grad_attention = contract_last(grad_out_all, values_all)
    grad_scores = (attention * (grad_attention - delta_rows[:, None]) * scale).astype(jnp.bfloat16)
    start = me_x * n_rows
    own_rows = lax.dynamic_slice_in_dim(grad_scores, start, n_rows, axis=0)
    own_cols = lax.dynamic_slice_in_dim(grad_scores, start, n_rows, axis=1)
    own_attention = lax.dynamic_slice_in_dim(attention_low, start, n_rows, axis=1)
    grad_query = jnp.dot(own_rows, keys_all, preferred_element_type=jnp.float32)
    grad_key = contract_first(own_cols, query_all)
    grad_value = contract_first(own_attention, grad_out_all)
    grad_heads = jnp.concatenate([grad_query, grad_key, grad_value], axis=1).astype(jnp.bfloat16)

    g_lo = grad_heads[:, :half]
    g_hi = grad_heads[:, half:]
    g_mine = jnp.where(first, g_lo, g_hi)
    g_other = jnp.where(first, g_hi, g_lo)

    def finish_input(parts):
        gm, go, wm, wo = parts
        return (contract_last(gm, wm) + contract_last(go, wo)).astype(jnp.bfloat16)

    input_parts = (g_mine, g_other, w_mine_all, w_other_all)

    wg_other = jnp.einsum("pyzd,pc->zydc", blocked, g_other, preferred_element_type=jnp.float32)
    wg_from_partner = dp_partner(wg_other.astype(jnp.bfloat16), 1)
    wg_mine = jnp.einsum("pyzd,pc->zydc", blocked, g_mine, preferred_element_type=jnp.float32)
    wg_mine, wg_from_partner = lax.optimization_barrier((wg_mine, wg_from_partner))
    blocks = wg_mine + wg_from_partner.astype(jnp.float32)
    over_z, input_grad = ring_reduce_scatter(blocks, ring_z, axis=0, beside=(input_parts, finish_input))
    over_fsdp, _ = ring_reduce_scatter(over_z, ring_y)

    by_seq = lax.all_gather(over_fsdp, "seq", axis=0, tiled=False)
    over_seq = by_seq[0]
    for s_i in range(1, by_seq.shape[0]):
        over_seq = over_seq + by_seq[s_i]
    by_dp = lax.all_gather(over_seq, "dp", axis=0, tiled=False)
    halves = []
    for c in range(2):
        part = by_dp[c]
        for d in range(c + 2, by_dp.shape[0], 2):
            part = part + by_dp[d]
        halves.append(part)
    weight_grad = jnp.concatenate(halves, axis=1)
    return (input_grad[None], weight_grad)


def inner_ring_size(mesh):
    axis = mesh.axis_names.index("fsdp")
    line = mesh.devices[tuple(0 if a != axis else slice(None) for a in range(mesh.devices.ndim))]
    line = list(line)
    if not hasattr(line[0], "coords"):
        return len(line)
    count = 1
    while count < len(line) and line[count].coords[1] == line[0].coords[1]:
        count += 1
    return count


def solution(mesh):
    inner = inner_ring_size(mesh)
    sizes = dict(zip(mesh.axis_names, mesh.devices.shape))
    split = jax.sharding.Mesh(
        mesh.devices.reshape(sizes["dp"], sizes["seq"], sizes["fsdp"] // inner, inner),
        ("dp", "seq", "fh", "fz"),
    )
    rows = ("dp", "fh", "fz")
    placed = (
        P(rows, "seq", None),
        P(rows, "seq"),
        P(("fh", "fz"), None),
        P(rows, "seq", None),
    )
    return jax.shard_map(
        functools.partial(shards, inner_fsdp=inner),
        mesh=split,
        in_specs=placed,
        out_specs=(P(rows, "seq", None), P(("fh", "fz"), None)),
        check_vma=False,
    )
```

```python
import functools

import jax
import jax.numpy as jnp
from jax import lax
from jax.sharding import PartitionSpec as P


def contract_first(left, right):
    return lax.dot_general(
        left, right, (((0,), (0,)), ((), ())), preferred_element_type=jnp.float32
    )


def contract_last(left, right):
    return lax.dot_general(
        left, right, (((1,), (1,)), ((), ())), preferred_element_type=jnp.float32
    )


def dp_partner(x, bit):
    pairs = [(i, i ^ bit) for i in range(lax.axis_size("dp"))]
    return lax.ppermute(x, "dp", perm=pairs)


class Ring:
    def __init__(self, axis, size, inner):
        self.axis, self.size, self.inner = axis, size, inner

    def total(self):
        return lax.axis_size(self.axis)

    def position(self):
        return (lax.axis_index(self.axis) // self.inner) % self.size

    def shift(self, x, step):
        n, inner, total = self.size, self.inner, self.total()
        pairs = []
        for i in range(total):
            pos = (i // inner) % n
            base = i - pos * inner
            pairs.append((i, base + ((pos + step) % n) * inner))
        return lax.ppermute(x, self.axis, perm=pairs)


def ring_gather(x, ring, beside=None, late=None):
    n = ring.size
    got, slot = [x], {0: 0}
    cw, ccw = x, x
    last_cw = n - 1 if (n - 1) % 2 == 1 else n - 2
    last_ccw = n - 1 if (n - 1) % 2 == 0 else n - 2
    for t in range(1, n):
        if t % 2 == 1:
            cw = ring.shift(cw, 1)
            if t == 1 and beside is not None:
                cw, beside = lax.optimization_barrier((cw, beside))
            if t == last_cw and late is not None:
                cw, late = lax.optimization_barrier((cw, late))
            slot[(n - (t + 1) // 2) % n] = len(got)
            got.append(cw)
        else:
            ccw = ring.shift(ccw, -1)
            if t == last_ccw and late is not None:
                value, make = late
                ccw, value = lax.optimization_barrier((ccw, value))
                late = make(value)
            slot[t // 2] = len(got)
            got.append(ccw)
    if late is not None:
        return jnp.stack(got), [slot[k] for k in range(n)], late
    return jnp.stack(got), [slot[k] for k in range(n)], beside


def ring_reduce_scatter(blocks, ring, axis=0, beside=None):
    n = ring.size
    me = ring.position()

    def pick(index):
        return lax.dynamic_index_in_dim(blocks, index % n, axis=axis, keepdims=False)

    total = pick(me)
    if n == 1:
        return total, beside
    up, down = n // 2, (n - 1) // 2
    acc = pick(me + up)
    for t in range(1, up + 1):
        acc = ring.shift(acc.astype(jnp.bfloat16), 1)
        acc = acc.astype(jnp.float32)
        if t < up:
            acc = acc + pick(me + up - t)
    total = total + acc
    if down:
        acc = pick(me - down)
        for t in range(1, down + 1):
            acc = ring.shift(acc.astype(jnp.bfloat16), -1)
            if t == 1 and beside is not None and down > 1:
                value, make = beside
                acc, value = lax.optimization_barrier((acc, value))
                beside = make(value)
            if t == 2 and beside is not None:
                acc, beside = lax.optimization_barrier((acc, beside))
            acc = acc.astype(jnp.float32)
            if t < down:
                acc = acc + pick(me - down + t)
        total = total + acc
    return total, beside


def shards(patches, segments, qkv_weight, cotangent, inner_fsdp):
    features = patches[0]
    image_ids = segments[0]
    grad_out = cotangent[0]
    width_head = cotangent.shape[2]
    width_all = qkv_weight.shape[1]
    rows_w = qkv_weight.shape[0]
    half = width_all // 2
    scale = width_head ** (-0.5)
    core = lax.axis_index("dp") % 2
    first = core == 0
    outer_fsdp = lax.axis_size("fh")
    n_fsdp = outer_fsdp * inner_fsdp
    ring_y = Ring("fh", outer_fsdp, 1)
    ring_z = Ring("fz", inner_fsdp, 1)
    ring_x = Ring("seq", lax.axis_size("seq"), 1)

    w_mine = lax.dynamic_slice_in_dim(qkv_weight, core * half, half, axis=1)
    stack_y = lax.all_gather(w_mine, "fh", axis=0, tiled=False)
    relayout = lambda f: f.reshape(f.shape[0], outer_fsdp, inner_fsdp, rows_w)
    stack_zy, slot_z, blocked = ring_gather(stack_y, ring_z, late=(features, relayout))
    flat = stack_zy.reshape(-1, rows_w, half)
    me_y, me_z = ring_y.position(), ring_z.position()
    absolute = jnp.arange(n_fsdp, dtype=jnp.int32)
    rel_z = (absolute % inner_fsdp - me_z) % inner_fsdp
    order = jnp.asarray(slot_z, jnp.int32)[rel_z] * outer_fsdp + absolute // inner_fsdp
    w_mine_all = jnp.take(flat, order, axis=0, mode="clip").reshape(n_fsdp * rows_w, half)
    w_other_all = dp_partner(w_mine_all, 1)

    h_mine = jnp.dot(features, w_mine_all, preferred_element_type=jnp.float32)
    h_other = jnp.dot(features, w_other_all, preferred_element_type=jnp.float32)
    projected = jnp.where(
        first,
        jnp.concatenate([h_mine, h_other], axis=1),
        jnp.concatenate([h_other, h_mine], axis=1),
    )
    heads = projected.astype(jnp.bfloat16)
    n_rows = features.shape[0]
    n_x = ring_x.size
    me_x = ring_x.position()
    ids_col = jnp.broadcast_to(image_ids.astype(jnp.bfloat16)[:, None], (n_rows, width_head))
    packed = jnp.concatenate([heads, grad_out, ids_col], axis=1)
    packed_all = lax.all_gather(packed, "seq", axis=0, tiled=True)
    query_all = packed_all[:, :width_head]
    keys_all = packed_all[:, width_head : 2 * width_head]
    values_all = packed_all[:, 2 * width_head : 3 * width_head]
    grad_out_all = packed_all[:, 3 * width_head : 4 * width_head]
    images_all = packed_all[:, 4 * width_head]
    scores = contract_last(query_all, keys_all) * scale
    allowed = images_all[:, None] == images_all[None, :]
    highest = jnp.max(jnp.where(allowed, scores, -jnp.inf), axis=1)
    summed = jnp.sum(jnp.where(allowed, jnp.exp(scores - highest[:, None]), 0.0), axis=1)
    log_total = highest + jnp.log(summed)
    attention = jnp.where(allowed, jnp.exp(scores - log_total[:, None]), 0.0)
    attention_low = attention.astype(jnp.bfloat16)
    output = jnp.dot(attention_low, values_all, preferred_element_type=jnp.float32)
    delta_rows = jnp.sum(grad_out_all.astype(jnp.float32) * output, axis=1)
    grad_attention = contract_last(grad_out_all, values_all)
    grad_scores = (attention * (grad_attention - delta_rows[:, None]) * scale).astype(jnp.bfloat16)
    start = me_x * n_rows
    own_rows = lax.dynamic_slice_in_dim(grad_scores, start, n_rows, axis=0)
    own_cols = lax.dynamic_slice_in_dim(grad_scores, start, n_rows, axis=1)
    own_attention = lax.dynamic_slice_in_dim(attention_low, start, n_rows, axis=1)
    grad_query = jnp.dot(own_rows, keys_all, preferred_element_type=jnp.float32)
    grad_key = contract_first(own_cols, query_all)
    grad_value = contract_first(own_attention, grad_out_all)
    grad_heads = jnp.concatenate([grad_query, grad_key, grad_value], axis=1).astype(jnp.bfloat16)

    g_lo = grad_heads[:, :half]
    g_hi = grad_heads[:, half:]
    g_mine = jnp.where(first, g_lo, g_hi)
    g_other = jnp.where(first, g_hi, g_lo)

    def finish_input(parts):
        gm, go, wm, wo = parts
        return (contract_last(gm, wm) + contract_last(go, wo)).astype(jnp.bfloat16)

    input_parts = (g_mine, g_other, w_mine_all, w_other_all)

    wg_other = jnp.einsum("pyzd,pc->zydc", blocked, g_other, preferred_element_type=jnp.float32)
    wg_from_partner = dp_partner(wg_other.astype(jnp.bfloat16), 1)
    wg_mine = jnp.einsum("pyzd,pc->zydc", blocked, g_mine, preferred_element_type=jnp.float32)
    wg_mine, wg_from_partner = lax.optimization_barrier((wg_mine, wg_from_partner))
    blocks = wg_mine + wg_from_partner.astype(jnp.float32)
    over_z, input_grad = ring_reduce_scatter(blocks, ring_z, axis=0, beside=(input_parts, finish_input))
    if isinstance(input_grad, tuple):
        input_grad = input_grad[1](input_grad[0])
    over_fsdp, _ = ring_reduce_scatter(over_z, ring_y)

    by_seq = lax.all_gather(over_fsdp, "seq", axis=0, tiled=False)
    over_seq = by_seq[0]
    for s_i in range(1, by_seq.shape[0]):
        over_seq = over_seq + by_seq[s_i]
    by_dp = lax.all_gather(over_seq, "dp", axis=0, tiled=False)
    halves = []
    for c in range(2):
        part = by_dp[c]
        for d in range(c + 2, by_dp.shape[0], 2):
            part = part + by_dp[d]
        halves.append(part)
    weight_grad = jnp.concatenate(halves, axis=1)
    return (input_grad[None], weight_grad)


def inner_ring_size(mesh):
    axis = mesh.axis_names.index("fsdp")
    line = mesh.devices[tuple(0 if a != axis else slice(None) for a in range(mesh.devices.ndim))]
    line = list(line)
    if not hasattr(line[0], "coords"):
        return len(line)
    count = 1
    while count < len(line) and line[count].coords[1] == line[0].coords[1]:
        count += 1
    return count


def solution(mesh):
    inner = inner_ring_size(mesh)
    sizes = dict(zip(mesh.axis_names, mesh.devices.shape))
    split = jax.sharding.Mesh(
        mesh.devices.reshape(sizes["dp"], sizes["seq"], sizes["fsdp"] // inner, inner),
        ("dp", "seq", "fh", "fz"),
    )
    rows = ("dp", "fh", "fz")
    placed = (
        P(rows, "seq", None),
        P(rows, "seq"),
        P(("fh", "fz"), None),
        P(rows, "seq", None),
    )
    return jax.shard_map(
        functools.partial(shards, inner_fsdp=inner),
        mesh=split,
        in_specs=placed,
        out_specs=(P(rows, "seq", None), P(("fh", "fz"), None)),
        check_vma=False,
    )
```
